512 devices in a mesh: tile: 64 (over x, y, z_hi, core), exp: 8 (over z_lo).
Axes of the slice: x: 4, y: 4, z: 16 (z_hi: 2, z_lo: 8; z = z_hi * 8 + z_lo), core: 2. Of those that a mesh axis runs over, the one named last changes fastest.
Arguments:
- initial: float32 [3, 16384, 256], P(None, ('exp', 'tile')), parts along dimension 1, may hold values from -6 to 6
- depth_field: float32 [16384, 256], P(('exp', 'tile')), parts along dimension 0, may hold values from 0.5 to 2
- coriolis: float32 [16384, 256], P(('exp', 'tile')), parts along dimension 0, may hold values from -1 to 1
- cell_area: float32 [16384, 256], P(('exp', 'tile')), parts along dimension 0, may hold values from 1 to 2
- face_len: float32 [2, 16384, 256], P(None, ('exp', 'tile')), parts along dimension 1, may hold values from 0.5 to 1
- owners: int32 [32768, 2], P(('exp', 'tile')), parts along dimension 0, may hold values from 0 to 63, as said below
- offsets: int32 [32768, 2], P(('exp', 'tile')), parts along dimension 0, may hold values from 0 to 15
- weights: bfloat16 [32768, 2, 128, 128], P(('exp', 'tile')), parts along dimension 0, may hold values from -0.25 to 0.25
Outputs:
- remapped: float32 [8192, 4, 128], P(('exp', 'tile')), parts along dimension 0
- final_fields: float32 [3, 16384, 256], P(None, ('exp', 'tile')), parts along dimension 1
The draws below stay inside these ranges and needn't reach their ends.
There are 8 independent parts, one for each index of `exp`. The reference program is written for one: setup_inputs(seed, part) draws one part's arguments, and reference() takes and returns one part's arrays. A program takes and returns all parts, laid end to end along the dimension named above; each array names one. Nothing has to cross between parts.
Inputs may be any that keep to these rules, and one draw needn't show every extreme that they name: `owners`: of the 128 intersections of one device's source blocks, at most 4 name the same owner; in every draw one owner is named by exactly 4 intersections of every device.
All inputs are finite; a program needn't handle non-finite values.
Results may differ from the reference program's by a relative error of at most 0.0029.
Values sent between devices are 32-bit elements; how exact they have to be, the bound alone decides.
No kernel may reach another device: no remote copies, remote signals or barrier semaphores. Data moves between devices by JAX's collectives and lax.ppermute only.
A program may use at most 64 MiB of HBM per device.

```python
import math
import jax
import jax.numpy as jnp

NY = 256
STEPS = 4
R = 2
TB = 16
SBLK = 64
CAP = 4
NX = 2048
SOURCE_BLOCKS = 4096
TBLOCKS = 1024
N_TILE = 64


def draw_owners(key, part):
    favored = jax.random.randint(jax.random.fold_in(key, 7), (), 0, N_TILE)
    items_all = jnp.arange(N_TILE * CAP, dtype=jnp.int32)
    owner_of = items_all // CAP
    rank_of = items_all % CAP

    def device_owners(device):
        device_key = jax.random.fold_in(key, device)
        ceiling = jax.random.randint(jax.random.fold_in(device_key, 1), (N_TILE,), CAP // 2, CAP + 1)
        ceiling = jnp.where(jnp.arange(N_TILE) == favored, CAP, ceiling)
        tiebreak = jax.random.permutation(jax.random.fold_in(device_key, 2), N_TILE * CAP)
        grades = jnp.where(owner_of == favored, 0, jnp.where(rank_of < ceiling[owner_of], 1, 2))
        ordering = jnp.argsort(grades * (N_TILE * CAP) + tiebreak)
        picked = ordering[:SBLK * R]
        picked = picked[jax.random.permutation(jax.random.fold_in(device_key, 3), SBLK * R)]
        return (picked // CAP).astype(jnp.int32).reshape(SBLK, R)
    return jax.vmap(device_owners)(jnp.arange(N_TILE)).reshape(N_TILE * SBLK, R)


def plant(array, stream_key, least, largest):
    longest = array.shape.index(max(array.shape))
    spots = []
    for shift in (0, 1):
        where = [jax.random.randint(jax.random.fold_in(stream_key, axis), (), 0, length) for axis, length in enumerate(array.shape)]
        where[longest] = (where[longest] + shift) % array.shape[longest]
        spots.append(tuple(where))
    return array.at[spots[0]].set(least).at[spots[1]].set(largest)


def level_of(stream_key, shape, cuts, smallest, high):
    level = 1.0
    for dim, blocks in cuts:
        steps = jax.random.uniform(jax.random.fold_in(jax.random.fold_in(stream_key, 6), dim), (blocks,), jnp.float32, smallest / len(cuts), high / len(cuts))
        level = level * jnp.repeat(jnp.exp(steps), shape[dim] // blocks).reshape((-1,) + (1,) * (len(shape) - 1 - dim))
    return level


def gaussian(own_key, extent, spread, most, cuts=(), kind=jnp.bfloat16):
    factor_of = level_of(own_key, extent, cuts, -0.22, 0.18) if cuts else 1.0
    result = jax.random.normal(own_key, extent, jnp.float32) * spread * factor_of
    return jnp.minimum(jnp.maximum(result, -most), most).astype(kind)


def setup_inputs(seed: int = 0, part: int = 0) -> dict:
    arg_keys = jax.random.split(jax.random.key(seed), 9)
    own_keys = jax.random.split(jax.random.fold_in(arg_keys[8], part), 9)
    initial = gaussian(own_keys[0], (3, NX, NY), 1.0, 6.0, ((1, 64),), jnp.float32)
    depth_field = jnp.clip(jnp.exp(math.log(2.0) - 1.3862944 * jax.random.uniform(own_keys[1], (NX, NY), jnp.float32) ** level_of(own_keys[1], (NX, NY), ((0, 64),), -0.2, 0.2)), 0.5, 2.0)
    coriolis = jnp.clip(jax.random.uniform(own_keys[2], (NX, NY), jnp.float32, -1.0, 1.0) * level_of(own_keys[2], (NX, NY), ((0, 64),), -0.4, 0.0), -1.0, 1.0)
    cell_area = jnp.clip(1.0 + 1.0 * jax.random.uniform(own_keys[3], (NX, NY), jnp.float32) ** level_of(own_keys[3], (NX, NY), ((0, 64),), -0.2, 0.2), 1.0, 2.0)
    face_len = jnp.clip(0.5 + 0.5 * jax.random.uniform(own_keys[4], (2, NX, NY), jnp.float32) ** level_of(own_keys[4], (2, NX, NY), ((1, 64),), -0.2, 0.2), 0.5, 1.0)
    owners = draw_owners(jax.random.fold_in(jax.random.fold_in(arg_keys[8], part), 71), part)
    offsets = plant(jax.random.randint(own_keys[6], (SOURCE_BLOCKS, R), 0, TB), jax.random.fold_in(own_keys[6], 1), 0, TB - 1).astype(jnp.int32)
    weights = gaussian(own_keys[7], (SOURCE_BLOCKS, R, 128, 128), 512 ** -0.5, 0.25, ((0, 64),))
    return dict(initial=initial, depth_field=depth_field, coriolis=coriolis, cell_area=cell_area, face_len=face_len, owners=owners, offsets=offsets, weights=weights)


time_step = 0.3

def wrapped(values, width):
    return jnp.concatenate([values[:, -width:], values, values[:, :width]], axis=1)

def advance(fields, metric):
    height, speed_x, speed_y = (fields[0], fields[1], fields[2])
    depth, rotation, area, east_len, north_len = (metric[0], metric[1], metric[2], metric[3], metric[4])
    wave_x = jnp.sqrt(jnp.maximum(depth[:-1], depth[1:]))
    edge = east_len[:-1]
    flux_h = edge * (0.5 * (depth[:-1] * speed_x[:-1] + depth[1:] * speed_x[1:]) - 0.5 * wave_x * (height[1:] - height[:-1]))
    flux_u = edge * (0.5 * (height[:-1] + height[1:]) - 0.5 * wave_x * (speed_x[1:] - speed_x[:-1]))
    flux_v = edge * (-0.5 * wave_x * (speed_y[1:] - speed_y[:-1]))
    own_h = height[1:-1]
    own_u = speed_x[1:-1]
    own_v = speed_y[1:-1]
    own_d = depth[1:-1]
    own_f = rotation[1:-1]
    own_a = area[1:-1]
    own_n = north_len[1:-1]
    above_h = jnp.concatenate([own_h[:, 1:], own_h[:, -1:]], axis=1)
    above_u = jnp.concatenate([own_u[:, 1:], own_u[:, -1:]], axis=1)
    above_v = jnp.concatenate([own_v[:, 1:], -own_v[:, -1:]], axis=1)
    above_d = jnp.concatenate([own_d[:, 1:], own_d[:, -1:]], axis=1)
    wave_y = jnp.sqrt(jnp.maximum(own_d, above_d))
    north_h = own_n * (0.5 * (own_d * own_v + above_d * above_v) - 0.5 * wave_y * (above_h - own_h))
    north_u = own_n * (-0.5 * wave_y * (above_u - own_u))
    north_v = own_n * (0.5 * (own_h + above_h) - 0.5 * wave_y * (above_v - own_v))
    wall_v = own_n[:, :1] * (own_h[:, :1] - jnp.sqrt(own_d[:, :1]) * own_v[:, :1])
    zeros = jnp.zeros_like(wall_v)
    south_h = jnp.concatenate([zeros, north_h[:, :-1]], axis=1)
    south_u = jnp.concatenate([zeros, north_u[:, :-1]], axis=1)
    south_v = jnp.concatenate([wall_v, north_v[:, :-1]], axis=1)
    factor = time_step / own_a
    new_h = own_h - factor * (flux_h[1:] - flux_h[:-1] + north_h - south_h)
    new_u = own_u - factor * (flux_u[1:] - flux_u[:-1] + north_u - south_u) + time_step * own_f * own_v
    new_v = own_v - factor * (flux_v[1:] - flux_v[:-1] + north_v - south_v) - time_step * own_f * own_u
    return jnp.stack([new_h, new_u, new_v])

def reference(initial, depth_field, coriolis, cell_area, face_len, owners, offsets, weights):
    metric = jnp.stack([depth_field, coriolis, cell_area, face_len[0], face_len[1]])
    metric_ext = wrapped(metric, 1)
    fields = initial
    snapshots = []
    for number in range(STEPS):
        fields = advance(wrapped(fields, 1), metric_ext)
        snapshots.append(fields[0])
    snapped = jnp.stack(snapshots).astype(jnp.bfloat16)
    blocks = snapped.reshape(STEPS, SOURCE_BLOCKS, 128).astype(jnp.float32)
    contribution = jnp.einsum('sbk,brkt->brst', blocks, weights.astype(jnp.float32))
    target = (owners * TB + offsets).reshape(-1).astype(jnp.int32)
    summed = jax.ops.segment_sum(contribution.reshape(SOURCE_BLOCKS * R, STEPS * 128), target, num_segments=TBLOCKS)
    return (summed.reshape(TBLOCKS, STEPS, 128), fields)
```

```python
import jax
import jax.numpy as jnp
from jax import lax
from jax.sharding import PartitionSpec as P

STEPS = 4
TB = 16
CAP = 4


time_step = 0.3


def with_halo(cells, sides, width):
    for axis, dim in sides:
        count = lax.axis_size(axis)
        head = lax.slice_in_dim(cells, 0, width, axis=dim)
        tail = lax.slice_in_dim(cells, cells.shape[dim] - width, cells.shape[dim], axis=dim)
        cells = jnp.concatenate(
            [
                lax.ppermute(tail, axis, [(i, (i + 1) % count) for i in range(count)]),
                cells,
                lax.ppermute(head, axis, [((i + 1) % count, i) for i in range(count)]),
            ],
            axis=dim,
        )
    return cells


def advance(fields, metric):
    height, speed_x, speed_y = (fields[0], fields[1], fields[2])
    depth, rotation, area, east_len, north_len = (
        metric[0],
        metric[1],
        metric[2],
        metric[3],
        metric[4],
    )
    wave_x = jnp.sqrt(jnp.maximum(depth[:-1], depth[1:]))
    edge = east_len[:-1]
    flux_h = edge * (
        0.5 * (depth[:-1] * speed_x[:-1] + depth[1:] * speed_x[1:])
        - 0.5 * wave_x * (height[1:] - height[:-1])
    )
    flux_u = edge * (0.5 * (height[:-1] + height[1:]) - 0.5 * wave_x * (speed_x[1:] - speed_x[:-1]))
    flux_v = edge * (-0.5 * wave_x * (speed_y[1:] - speed_y[:-1]))
    own_h = height[1:-1]
    own_u = speed_x[1:-1]
    own_v = speed_y[1:-1]
    own_d = depth[1:-1]
    own_f = rotation[1:-1]
    own_a = area[1:-1]
    own_n = north_len[1:-1]
    above_h = jnp.concatenate([own_h[:, 1:], own_h[:, -1:]], axis=1)
    above_u = jnp.concatenate([own_u[:, 1:], own_u[:, -1:]], axis=1)
    above_v = jnp.concatenate([own_v[:, 1:], -own_v[:, -1:]], axis=1)
    above_d = jnp.concatenate([own_d[:, 1:], own_d[:, -1:]], axis=1)
    wave_y = jnp.sqrt(jnp.maximum(own_d, above_d))
    north_h = own_n * (0.5 * (own_d * own_v + above_d * above_v) - 0.5 * wave_y * (above_h - own_h))
    north_u = own_n * (-0.5 * wave_y * (above_u - own_u))
    north_v = own_n * (0.5 * (own_h + above_h) - 0.5 * wave_y * (above_v - own_v))
    wall_v = own_n[:, :1] * (own_h[:, :1] - jnp.sqrt(own_d[:, :1]) * own_v[:, :1])
    zeros = jnp.zeros_like(wall_v)
    south_h = jnp.concatenate([zeros, north_h[:, :-1]], axis=1)
    south_u = jnp.concatenate([zeros, north_u[:, :-1]], axis=1)
    south_v = jnp.concatenate([wall_v, north_v[:, :-1]], axis=1)
    factor = time_step / own_a
    new_h = own_h - factor * (flux_h[1:] - flux_h[:-1] + north_h - south_h)
    new_u = (
        own_u - factor * (flux_u[1:] - flux_u[:-1] + north_u - south_u) + time_step * own_f * own_v
    )
    new_v = (
        own_v - factor * (flux_v[1:] - flux_v[:-1] + north_v - south_v) - time_step * own_f * own_u
    )
    return jnp.stack([new_h, new_u, new_v])


def on_device(initial, depth_field, coriolis, cell_area, face_len, owners, offsets, weights):
    metric = jnp.concatenate([jnp.stack([depth_field, coriolis, cell_area]), face_len], axis=0)
    snapshots = []
    metric_ext = with_halo(metric, (("tile", 1),), 1)
    fields = initial
    for number in range(STEPS):
        fields = advance(with_halo(fields, (("tile", 1),), 1), metric_ext)
        snapshots.append(fields[0])
    snapped = jnp.stack(snapshots).astype(jnp.bfloat16).reshape(STEPS, -1, 128)
    contribution = jnp.einsum(
        "sbk,brkt->brst", snapped, weights, preferred_element_type=jnp.float32
    )
    slot_count = weights.shape[0] * weights.shape[1]
    flat = contribution.reshape(slot_count, STEPS * 128)
    n_tile = lax.axis_size("tile")
    me = lax.axis_index("tile")
    labels = jnp.concatenate([owners.reshape(1, -1), offsets.reshape(1, -1)], axis=0)
    all_labels = lax.all_gather(labels, "tile", axis=0, tiled=False)
    all_owner = all_labels[:, 0]
    all_offset = all_labels[:, 1]
    item = jnp.arange(slot_count, dtype=jnp.int32)
    earlier = item[None, :] < item[:, None]

    def rank_of(owner_list):
        same = owner_list[:, None] == owner_list[None, :]
        return jnp.sum((same & earlier).astype(jnp.int32), axis=1)

    own_owner = owners.reshape(-1)
    slot = own_owner * CAP + rank_of(own_owner)
    pack = (jnp.arange(n_tile * CAP, dtype=jnp.int32)[:, None] == slot[None, :]).astype(
        jnp.float32
    )
    send = jnp.dot(pack, flat, precision=lax.Precision.HIGHEST, preferred_element_type=jnp.float32)
    recv = lax.all_to_all(
        send.reshape(n_tile, CAP * STEPS * 128), "tile", 0, 0, tiled=True
    ).reshape(n_tile * CAP, STEPS * 128)
    ranks = jax.vmap(rank_of)(all_owner)
    mine = all_owner == me
    hit_t = (all_offset[:, :, None] == jnp.arange(TB, dtype=jnp.int32)) & mine[:, :, None]
    hit_r = ranks[:, :, None] == jnp.arange(CAP, dtype=jnp.int32)
    unpack = jnp.einsum(
        "djt,djr->tdr", hit_t.astype(jnp.float32), hit_r.astype(jnp.float32)
    ).reshape(TB, n_tile * CAP)
    gathered = jnp.dot(
        unpack, recv, precision=lax.Precision.HIGHEST, preferred_element_type=jnp.float32
    )
    return (gathered.reshape(TB, STEPS, 128), fields)


def solution(mesh):
    placed = (
        P(None, ("exp", "tile"), None),
        P(("exp", "tile"), None),
        P(("exp", "tile"), None),
        P(("exp", "tile"), None),
        P(None, ("exp", "tile"), None),
        P(("exp", "tile"), None),
        P(("exp", "tile"), None),
        P(("exp", "tile"), None, None, None),
    )
    return jax.shard_map(
        on_device,
        mesh=mesh,
        in_specs=placed,
        out_specs=(P(("exp", "tile"), None, None), P(None, ("exp", "tile"), None)),
        check_vma=False,
    )
```

```python
import jax
import jax.numpy as jnp
from jax import lax
from jax.sharding import PartitionSpec as P

STEPS = 4
TB = 16
CAP = 4


time_step = 0.3


def with_halo(cells, sides, width):
    for axis, dim in sides:
        count = lax.axis_size(axis)
        head = lax.slice_in_dim(cells, 0, width, axis=dim)
        tail = lax.slice_in_dim(cells, cells.shape[dim] - width, cells.shape[dim], axis=dim)
        cells = jnp.concatenate(
            [
                lax.ppermute(tail, axis, [(i, (i + 1) % count) for i in range(count)]),
                cells,
                lax.ppermute(head, axis, [((i + 1) % count, i) for i in range(count)]),
            ],
            axis=dim,
        )
    return cells


def advance(fields, metric):
    height, speed_x, speed_y = (fields[0], fields[1], fields[2])
    depth, rotation, area, east_len, north_len = (
        metric[0],
        metric[1],
        metric[2],
        metric[3],
        metric[4],
    )
    wave_x = jnp.sqrt(jnp.maximum(depth[:-1], depth[1:]))
    edge = east_len[:-1]
    flux_h = edge * (
        0.5 * (depth[:-1] * speed_x[:-1] + depth[1:] * speed_x[1:])
        - 0.5 * wave_x * (height[1:] - height[:-1])
    )
    flux_u = edge * (0.5 * (height[:-1] + height[1:]) - 0.5 * wave_x * (speed_x[1:] - speed_x[:-1]))
    flux_v = edge * (-0.5 * wave_x * (speed_y[1:] - speed_y[:-1]))
    own_h = height[1:-1]
    own_u = speed_x[1:-1]
    own_v = speed_y[1:-1]
    own_d = depth[1:-1]
    own_f = rotation[1:-1]
    own_a = area[1:-1]
    own_n = north_len[1:-1]
    above_h = jnp.concatenate([own_h[:, 1:], own_h[:, -1:]], axis=1)
    above_u = jnp.concatenate([own_u[:, 1:], own_u[:, -1:]], axis=1)
    above_v = jnp.concatenate([own_v[:, 1:], -own_v[:, -1:]], axis=1)
    above_d = jnp.concatenate([own_d[:, 1:], own_d[:, -1:]], axis=1)
    wave_y = jnp.sqrt(jnp.maximum(own_d, above_d))
    north_h = own_n * (0.5 * (own_d * own_v + above_d * above_v) - 0.5 * wave_y * (above_h - own_h))
    north_u = own_n * (-0.5 * wave_y * (above_u - own_u))
    north_v = own_n * (0.5 * (own_h + above_h) - 0.5 * wave_y * (above_v - own_v))
    wall_v = own_n[:, :1] * (own_h[:, :1] - jnp.sqrt(own_d[:, :1]) * own_v[:, :1])
    zeros = jnp.zeros_like(wall_v)
    south_h = jnp.concatenate([zeros, north_h[:, :-1]], axis=1)
    south_u = jnp.concatenate([zeros, north_u[:, :-1]], axis=1)
    south_v = jnp.concatenate([wall_v, north_v[:, :-1]], axis=1)
    factor = time_step / own_a
    new_h = own_h - factor * (flux_h[1:] - flux_h[:-1] + north_h - south_h)
    new_u = (
        own_u - factor * (flux_u[1:] - flux_u[:-1] + north_u - south_u) + time_step * own_f * own_v
    )
    new_v = (
        own_v - factor * (flux_v[1:] - flux_v[:-1] + north_v - south_v) - time_step * own_f * own_u
    )
    return jnp.stack([new_h, new_u, new_v])


def on_device(initial, depth_field, coriolis, cell_area, face_len, owners, offsets, weights):
    cells = jnp.concatenate(
        [initial, jnp.stack([depth_field, coriolis, cell_area]), face_len], axis=0
    )
    cells_ext = with_halo(cells, (("tile", 1),), STEPS)
    width = cells_ext.shape[1]
    fields = cells_ext[:3]
    snapshots = []
    for number in range(STEPS):
        metric_ext = cells_ext[3:, number : width - number]
        fields = advance(fields, metric_ext)
        keep = STEPS - 1 - number
        snapshots.append(fields[0, keep : fields.shape[1] - keep])
    snapped = jnp.stack(snapshots).astype(jnp.bfloat16).reshape(STEPS, -1, 128)
    contribution = jnp.einsum(
        "sbk,brkt->brst", snapped, weights, preferred_element_type=jnp.float32
    )
    slot_count = weights.shape[0] * weights.shape[1]
    flat = contribution.reshape(slot_count, STEPS * 128)
    n_tile = lax.axis_size("tile")
    item = jnp.arange(slot_count, dtype=jnp.int32)
    own_owner = owners.reshape(-1)
    same = own_owner[:, None] == own_owner[None, :]
    rank = jnp.sum((same & (item[None, :] < item[:, None])).astype(jnp.int32), axis=1)
    slot = own_owner * CAP + rank
    pack = (jnp.arange(n_tile * CAP, dtype=jnp.int32)[:, None] == slot[None, :]).astype(
        jnp.float32
    )
    send = jnp.dot(pack, flat, precision=lax.Precision.HIGHEST, preferred_element_type=jnp.float32)
    labels = jnp.dot(
        pack,
        offsets.reshape(-1, 1).astype(jnp.float32) + 1.0,
        precision=lax.Precision.HIGHEST,
        preferred_element_type=jnp.float32,
    ).reshape(n_tile, CAP) - 1.0
    label_row = jnp.pad(labels, ((0, 0), (0, 128 - CAP)))
    payload = jnp.concatenate([send.reshape(n_tile, CAP * STEPS * 128), label_row], axis=1)
    recv = lax.all_to_all(payload, "tile", 0, 0, tiled=True)
    recv_data = recv[:, : CAP * STEPS * 128].reshape(n_tile * CAP, STEPS * 128)
    recv_offset = recv[:, CAP * STEPS * 128 : CAP * STEPS * 128 + CAP].reshape(-1)
    unpack = (
        recv_offset[None, :] == jnp.arange(TB, dtype=jnp.float32)[:, None]
    ).astype(jnp.float32)
    gathered = jnp.dot(
        unpack, recv_data, precision=lax.Precision.HIGHEST, preferred_element_type=jnp.float32
    )
    return (gathered.reshape(TB, STEPS, 128), fields)


def solution(mesh):
    placed = (
        P(None, ("exp", "tile"), None),
        P(("exp", "tile"), None),
        P(("exp", "tile"), None),
        P(("exp", "tile"), None),
        P(None, ("exp", "tile"), None),
        P(("exp", "tile"), None),
        P(("exp", "tile"), None),
        P(("exp", "tile"), None, None, None),
    )
    return jax.shard_map(
        on_device,
        mesh=mesh,
        in_specs=placed,
        out_specs=(P(("exp", "tile"), None, None), P(None, ("exp", "tile"), None)),
        check_vma=False,
    )
```

```python
import jax
import jax.numpy as jnp
from jax import lax
from jax.sharding import PartitionSpec as P

STEPS = 4
TB = 16
CAP = 4


time_step = 0.3


def with_halo(cells, sides, width):
    for axis, dim in sides:
        count = lax.axis_size(axis)
        head = lax.slice_in_dim(cells, 0, width, axis=dim)
        tail = lax.slice_in_dim(cells, cells.shape[dim] - width, cells.shape[dim], axis=dim)
        if count % 2 == 0:
            odd = lax.axis_index(axis) % 2 == 1
            near = lax.ppermute(
                jnp.where(odd, head, tail), axis, [(i, i ^ 1) for i in range(count)]
            )
            far = lax.ppermute(
                jnp.where(odd, tail, head),
                axis,
                [(i, (i + 1) % count if i % 2 else (i - 1) % count) for i in range(count)],
            )
            before = jnp.where(odd, near, far)
            after = jnp.where(odd, far, near)
        else:
            before = lax.ppermute(tail, axis, [(i, (i + 1) % count) for i in range(count)])
            after = lax.ppermute(head, axis, [((i + 1) % count, i) for i in range(count)])
        cells = jnp.concatenate([before, cells, after], axis=dim)
    return cells


def advance(fields, metric):
    height, speed_x, speed_y = (fields[0], fields[1], fields[2])
    depth, rotation, area, east_len, north_len = (
        metric[0],
        metric[1],
        metric[2],
        metric[3],
        metric[4],
    )
    wave_x = jnp.sqrt(jnp.maximum(depth[:-1], depth[1:]))
    edge = east_len[:-1]
    flux_h = edge * (
        0.5 * (depth[:-1] * speed_x[:-1] + depth[1:] * speed_x[1:])
        - 0.5 * wave_x * (height[1:] - height[:-1])
    )
    flux_u = edge * (0.5 * (height[:-1] + height[1:]) - 0.5 * wave_x * (speed_x[1:] - speed_x[:-1]))
    flux_v = edge * (-0.5 * wave_x * (speed_y[1:] - speed_y[:-1]))
    own_h = height[1:-1]
    own_u = speed_x[1:-1]
    own_v = speed_y[1:-1]
    own_d = depth[1:-1]
    own_f = rotation[1:-1]
    own_a = area[1:-1]
    own_n = north_len[1:-1]
    above_h = jnp.concatenate([own_h[:, 1:], own_h[:, -1:]], axis=1)
    above_u = jnp.concatenate([own_u[:, 1:], own_u[:, -1:]], axis=1)
    above_v = jnp.concatenate([own_v[:, 1:], -own_v[:, -1:]], axis=1)
    above_d = jnp.concatenate([own_d[:, 1:], own_d[:, -1:]], axis=1)
    wave_y = jnp.sqrt(jnp.maximum(own_d, above_d))
    north_h = own_n * (0.5 * (own_d * own_v + above_d * above_v) - 0.5 * wave_y * (above_h - own_h))
    north_u = own_n * (-0.5 * wave_y * (above_u - own_u))
    north_v = own_n * (0.5 * (own_h + above_h) - 0.5 * wave_y * (above_v - own_v))
    wall_v = own_n[:, :1] * (own_h[:, :1] - jnp.sqrt(own_d[:, :1]) * own_v[:, :1])
    zeros = jnp.zeros_like(wall_v)
    south_h = jnp.concatenate([zeros, north_h[:, :-1]], axis=1)
    south_u = jnp.concatenate([zeros, north_u[:, :-1]], axis=1)
    south_v = jnp.concatenate([wall_v, north_v[:, :-1]], axis=1)
    factor = time_step / own_a
    new_h = own_h - factor * (flux_h[1:] - flux_h[:-1] + north_h - south_h)
    new_u = (
        own_u - factor * (flux_u[1:] - flux_u[:-1] + north_u - south_u) + time_step * own_f * own_v
    )
    new_v = (
        own_v - factor * (flux_v[1:] - flux_v[:-1] + north_v - south_v) - time_step * own_f * own_u
    )
    return jnp.stack([new_h, new_u, new_v])


def on_device(initial, depth_field, coriolis, cell_area, face_len, owners, offsets, weights):
    cells = jnp.concatenate(
        [initial, jnp.stack([depth_field, coriolis, cell_area]), face_len], axis=0
    )
    cells_ext = with_halo(cells, (("tile", 1),), STEPS)
    width = cells_ext.shape[1]
    fields = cells_ext[:3]
    snapshots = []
    for number in range(STEPS):
        metric_ext = cells_ext[3:, number : width - number]
        fields = advance(fields, metric_ext)
        keep = STEPS - 1 - number
        snapshots.append(fields[0, keep : fields.shape[1] - keep])
    snapped = jnp.stack(snapshots).astype(jnp.bfloat16).reshape(STEPS, -1, 128)
    contribution = jnp.einsum(
        "sbk,brkt->brst", snapped, weights, preferred_element_type=jnp.float32
    )
    slot_count = weights.shape[0] * weights.shape[1]
    flat = contribution.reshape(slot_count, STEPS * 128)
    n_tile = lax.axis_size("tile")
    item = jnp.arange(slot_count, dtype=jnp.int32)
    own_owner = owners.reshape(-1)
    same = own_owner[:, None] == own_owner[None, :]
    rank = jnp.sum((same & (item[None, :] < item[:, None])).astype(jnp.int32), axis=1)
    slot = own_owner * CAP + rank
    pack = (jnp.arange(n_tile * CAP, dtype=jnp.int32)[:, None] == slot[None, :]).astype(
        jnp.float32
    )
    send = jnp.dot(pack, flat, precision=lax.Precision.HIGHEST, preferred_element_type=jnp.float32)
    labels = jnp.dot(
        pack,
        offsets.reshape(-1, 1).astype(jnp.float32) + 1.0,
        precision=lax.Precision.HIGHEST,
        preferred_element_type=jnp.float32,
    ).reshape(n_tile, CAP) - 1.0
    label_row = jnp.pad(labels, ((0, 0), (0, 128 - CAP)))
    payload = jnp.concatenate([send.reshape(n_tile, CAP * STEPS * 128), label_row], axis=1)
    recv = lax.all_to_all(payload, "tile", 0, 0, tiled=True)
    recv_data = recv[:, : CAP * STEPS * 128].reshape(n_tile * CAP, STEPS * 128)
    recv_offset = recv[:, CAP * STEPS * 128 : CAP * STEPS * 128 + CAP].reshape(-1)
    unpack = (
        recv_offset[None, :] == jnp.arange(TB, dtype=jnp.float32)[:, None]
    ).astype(jnp.float32)
    gathered = jnp.dot(
        unpack, recv_data, precision=lax.Precision.HIGHEST, preferred_element_type=jnp.float32
    )
    return (gathered.reshape(TB, STEPS, 128), fields)


def solution(mesh):
    placed = (
        P(None, ("exp", "tile"), None),
        P(("exp", "tile"), None),
        P(("exp", "tile"), None),
        P(("exp", "tile"), None),
        P(None, ("exp", "tile"), None),
        P(("exp", "tile"), None),
        P(("exp", "tile"), None),
        P(("exp", "tile"), None, None, None),
    )
    return jax.shard_map(
        on_device,
        mesh=mesh,
        in_specs=placed,
        out_specs=(P(("exp", "tile"), None, None), P(None, ("exp", "tile"), None)),
        check_vma=False,
    )
```

```python
import jax
import jax.numpy as jnp
from jax import lax
from jax.sharding import PartitionSpec as P

STEPS = 4
TB = 16
CAP = 4


time_step = 0.3


def halo_pair(head, tail, axis):
    count = lax.axis_size(axis)
    if count % 2 == 0:
        odd = lax.axis_index(axis) % 2 == 1
        near = lax.ppermute(jnp.where(odd, head, tail), axis, [(i, i ^ 1) for i in range(count)])
        far = lax.ppermute(
            jnp.where(odd, tail, head),
            axis,
            [(i, (i + 1) % count if i % 2 else (i - 1) % count) for i in range(count)],
        )
        return jnp.where(odd, near, far), jnp.where(odd, far, near)
    before = lax.ppermute(tail, axis, [(i, (i + 1) % count) for i in range(count)])
    after = lax.ppermute(head, axis, [((i + 1) % count, i) for i in range(count)])
    return before, after


def advance(fields, metric):
    height, speed_x, speed_y = (fields[0], fields[1], fields[2])
    depth, rotation, area, east_len, north_len = (
        metric[0],
        metric[1],
        metric[2],
        metric[3],
        metric[4],
    )
    wave_x = jnp.sqrt(jnp.maximum(depth[:-1], depth[1:]))
    edge = east_len[:-1]
    flux_h = edge * (
        0.5 * (depth[:-1] * speed_x[:-1] + depth[1:] * speed_x[1:])
        - 0.5 * wave_x * (height[1:] - height[:-1])
    )
    flux_u = edge * (0.5 * (height[:-1] + height[1:]) - 0.5 * wave_x * (speed_x[1:] - speed_x[:-1]))
    flux_v = edge * (-0.5 * wave_x * (speed_y[1:] - speed_y[:-1]))
    own_h = height[1:-1]
    own_u = speed_x[1:-1]
    own_v = speed_y[1:-1]
    own_d = depth[1:-1]
    own_f = rotation[1:-1]
    own_a = area[1:-1]
    own_n = north_len[1:-1]
    above_h = jnp.concatenate([own_h[:, 1:], own_h[:, -1:]], axis=1)
    above_u = jnp.concatenate([own_u[:, 1:], own_u[:, -1:]], axis=1)
    above_v = jnp.concatenate([own_v[:, 1:], -own_v[:, -1:]], axis=1)
    above_d = jnp.concatenate([own_d[:, 1:], own_d[:, -1:]], axis=1)
    wave_y = jnp.sqrt(jnp.maximum(own_d, above_d))
    north_h = own_n * (0.5 * (own_d * own_v + above_d * above_v) - 0.5 * wave_y * (above_h - own_h))
    north_u = own_n * (-0.5 * wave_y * (above_u - own_u))
    north_v = own_n * (0.5 * (own_h + above_h) - 0.5 * wave_y * (above_v - own_v))
    wall_v = own_n[:, :1] * (own_h[:, :1] - jnp.sqrt(own_d[:, :1]) * own_v[:, :1])
    zeros = jnp.zeros_like(wall_v)
    south_h = jnp.concatenate([zeros, north_h[:, :-1]], axis=1)
    south_u = jnp.concatenate([zeros, north_u[:, :-1]], axis=1)
    south_v = jnp.concatenate([wall_v, north_v[:, :-1]], axis=1)
    factor = time_step / own_a
    new_h = own_h - factor * (flux_h[1:] - flux_h[:-1] + north_h - south_h)
    new_u = (
        own_u - factor * (flux_u[1:] - flux_u[:-1] + north_u - south_u) + time_step * own_f * own_v
    )
    new_v = (
        own_v - factor * (flux_v[1:] - flux_v[:-1] + north_v - south_v) - time_step * own_f * own_u
    )
    return jnp.stack([new_h, new_u, new_v])


def on_device(initial, depth_field, coriolis, cell_area, face_len, owners, offsets, weights):
    pieces = [initial, depth_field[None], coriolis[None], cell_area[None], face_len]
    width = STEPS
    n_tile = lax.axis_size("tile")
    slot_count = weights.shape[0] * weights.shape[1]
    item = jnp.arange(slot_count, dtype=jnp.int32)
    own_owner = owners.reshape(-1)
    same = own_owner[:, None] == own_owner[None, :]
    rank = jnp.sum((same & (item[None, :] < item[:, None])).astype(jnp.int32), axis=1)
    slot = own_owner * CAP + rank
    pack = (jnp.arange(n_tile * CAP, dtype=jnp.int32)[:, None] == slot[None, :]).astype(
        jnp.float32
    )
    labels = jnp.dot(
        pack,
        offsets.reshape(-1, 1).astype(jnp.float32) + 1.0,
        precision=lax.Precision.HIGHEST,
        preferred_element_type=jnp.float32,
    ).reshape(n_tile, CAP) - 1.0
    label_row = jnp.pad(labels, ((0, 0), (0, 128 - CAP)))
    head = jnp.concatenate([p[:, :width] for p in pieces], axis=0)
    tail = jnp.concatenate([p[:, p.shape[1] - width :] for p in pieces], axis=0)
    head, tail, pack, label_row = lax.optimization_barrier((head, tail, pack, label_row))
    before, after = halo_pair(head, tail, "tile")
    cells_ext = jnp.concatenate([before, jnp.concatenate(pieces, axis=0), after], axis=1)
    full = cells_ext.shape[1]
    fields = cells_ext[:3]
    snapshots = []
    for number in range(STEPS):
        metric_ext = cells_ext[3:, number : full - number]
        fields = advance(fields, metric_ext)
        keep = STEPS - 1 - number
        snapshots.append(fields[0, keep : fields.shape[1] - keep])
    snapped = jnp.stack(snapshots).astype(jnp.bfloat16).reshape(STEPS, -1, 128)
    contribution = jnp.einsum(
        "sbk,brkt->brst", snapped, weights, preferred_element_type=jnp.float32
    )
    flat = contribution.reshape(slot_count, STEPS * 128)
    send = jnp.dot(pack, flat, precision=lax.Precision.HIGHEST, preferred_element_type=jnp.float32)
    payload = jnp.concatenate([send.reshape(n_tile, CAP * STEPS * 128), label_row], axis=1)
    recv = lax.all_to_all(payload, "tile", 0, 0, tiled=True)
    recv_data = recv[:, : CAP * STEPS * 128].reshape(n_tile * CAP, STEPS * 128)
    recv_offset = recv[:, CAP * STEPS * 128 : CAP * STEPS * 128 + CAP].reshape(-1)
    unpack = (
        recv_offset[None, :] == jnp.arange(TB, dtype=jnp.float32)[:, None]
    ).astype(jnp.float32)
    gathered = jnp.dot(
        unpack, recv_data, precision=lax.Precision.HIGHEST, preferred_element_type=jnp.float32
    )
    return (gathered.reshape(TB, STEPS, 128), fields)


def solution(mesh):
    placed = (
        P(None, ("exp", "tile"), None),
        P(("exp", "tile"), None),
        P(("exp", "tile"), None),
        P(("exp", "tile"), None),
        P(None, ("exp", "tile"), None),
        P(("exp", "tile"), None),
        P(("exp", "tile"), None),
        P(("exp", "tile"), None, None, None),
    )
    return jax.shard_map(
        on_device,
        mesh=mesh,
        in_specs=placed,
        out_specs=(P(("exp", "tile"), None, None), P(None, ("exp", "tile"), None)),
        check_vma=False,
    )
```

```python
import jax
import jax.numpy as jnp
from jax import lax
from jax.sharding import PartitionSpec as P
from jax.experimental import pallas as pl
from jax.experimental.pallas import tpu as pltpu

STEPS = 4
TB = 16
CAP = 4
HALO = 8
CHANNELS = 8


time_step = 0.3


def with_halo(cells, sides, width):
    for axis, dim in sides:
        count = lax.axis_size(axis)
        head = lax.slice_in_dim(cells, 0, width, axis=dim)
        tail = lax.slice_in_dim(cells, cells.shape[dim] - width, cells.shape[dim], axis=dim)
        if count % 2 == 0:
            odd = lax.axis_index(axis) % 2 == 1
            near = lax.ppermute(
                jnp.where(odd, head, tail), axis, [(i, i ^ 1) for i in range(count)]
            )
            far = lax.ppermute(
                jnp.where(odd, tail, head),
                axis,
                [(i, (i + 1) % count if i % 2 else (i - 1) % count) for i in range(count)],
            )
            before = jnp.where(odd, near, far)
            after = jnp.where(odd, far, near)
        else:
            before = lax.ppermute(tail, axis, [(i, (i + 1) % count) for i in range(count)])
            after = lax.ppermute(head, axis, [((i + 1) % count, i) for i in range(count)])
        cells = jnp.concatenate([before, cells, after], axis=dim)
    return cells


def advance(fields, metric):
    height, speed_x, speed_y = (fields[0], fields[1], fields[2])
    depth, rotation, area, east_len, north_len = (
        metric[0],
        metric[1],
        metric[2],
        metric[3],
        metric[4],
    )
    wave_x = jnp.sqrt(jnp.maximum(depth[:-1], depth[1:]))
    edge = east_len[:-1]
    flux_h = edge * (
        0.5 * (depth[:-1] * speed_x[:-1] + depth[1:] * speed_x[1:])
        - 0.5 * wave_x * (height[1:] - height[:-1])
    )
    flux_u = edge * (0.5 * (height[:-1] + height[1:]) - 0.5 * wave_x * (speed_x[1:] - speed_x[:-1]))
    flux_v = edge * (-0.5 * wave_x * (speed_y[1:] - speed_y[:-1]))
    own_h = height[1:-1]
    own_u = speed_x[1:-1]
    own_v = speed_y[1:-1]
    own_d = depth[1:-1]
    own_f = rotation[1:-1]
    own_a = area[1:-1]
    own_n = north_len[1:-1]
    above_h = jnp.concatenate([own_h[:, 1:], own_h[:, -1:]], axis=1)
    above_u = jnp.concatenate([own_u[:, 1:], own_u[:, -1:]], axis=1)
    above_v = jnp.concatenate([own_v[:, 1:], -own_v[:, -1:]], axis=1)
    above_d = jnp.concatenate([own_d[:, 1:], own_d[:, -1:]], axis=1)
    wave_y = jnp.sqrt(jnp.maximum(own_d, above_d))
    north_h = own_n * (0.5 * (own_d * own_v + above_d * above_v) - 0.5 * wave_y * (above_h - own_h))
    north_u = own_n * (-0.5 * wave_y * (above_u - own_u))
    north_v = own_n * (0.5 * (own_h + above_h) - 0.5 * wave_y * (above_v - own_v))
    wall_v = own_n[:, :1] * (own_h[:, :1] - jnp.sqrt(own_d[:, :1]) * own_v[:, :1])
    zeros = jnp.zeros_like(wall_v)
    south_h = jnp.concatenate([zeros, north_h[:, :-1]], axis=1)
    south_u = jnp.concatenate([zeros, north_u[:, :-1]], axis=1)
    south_v = jnp.concatenate([wall_v, north_v[:, :-1]], axis=1)
    factor = time_step / own_a
    new_h = own_h - factor * (flux_h[1:] - flux_h[:-1] + north_h - south_h)
    new_u = (
        own_u - factor * (flux_u[1:] - flux_u[:-1] + north_u - south_u) + time_step * own_f * own_v
    )
    new_v = (
        own_v - factor * (flux_v[1:] - flux_v[:-1] + north_v - south_v) - time_step * own_f * own_u
    )
    return jnp.stack([new_h, new_u, new_v])


def edge_kernel(odd_ref, ini_h, ini_t, dep_h, dep_t, cor_h, cor_t, area_h, area_t, face_h, face_t, near_ref, far_ref):
    odd = odd_ref[0] == 1
    head = [ini_h[0], ini_h[1], ini_h[2], dep_h[...], cor_h[...], area_h[...], face_h[0], face_h[1]]
    tail = [ini_t[0], ini_t[1], ini_t[2], dep_t[...], cor_t[...], area_t[...], face_t[0], face_t[1]]
    for c in range(CHANNELS):
        near_ref[c] = jnp.where(odd, head[c], tail[c])
        far_ref[c] = jnp.where(odd, tail[c], head[c])


def edges(odd, initial, depth_field, coriolis, cell_area, face_len):
    rows, lanes = depth_field.shape
    last = rows // HALO - 1
    spec3 = lambda b: pl.BlockSpec((3, HALO, lanes), lambda i: (0, b, 0))
    spec2 = lambda b: pl.BlockSpec((HALO, lanes), lambda i: (b, 0))
    specf = lambda b: pl.BlockSpec((2, HALO, lanes), lambda i: (0, b, 0))
    out = jax.ShapeDtypeStruct((CHANNELS, HALO, lanes), jnp.float32)
    return pl.pallas_call(
        edge_kernel,
        out_shape=(out, out),
        in_specs=[
            pl.BlockSpec(memory_space=pltpu.SMEM),
            spec3(0), spec3(last), spec2(0), spec2(last), spec2(0), spec2(last),
            spec2(0), spec2(last), specf(0), specf(last),
        ],
        out_specs=(
            pl.BlockSpec((CHANNELS, HALO, lanes), lambda i: (0, 0, 0)),
            pl.BlockSpec((CHANNELS, HALO, lanes), lambda i: (0, 0, 0)),
        ),
        grid=(1,),
    )(odd, initial, initial, depth_field, depth_field, coriolis, coriolis, cell_area, cell_area, face_len, face_len)


def stencil_kernel(ini, dep, cor, area, face, before, after, final_ref, snap_ref, ext):
    own_rows = ini.shape[1]
    owns = [ini[0], ini[1], ini[2], dep[...], cor[...], area[...], face[0], face[1]]
    for c in range(CHANNELS):
        ext[c, :HALO] = before[c]
        ext[c, HALO : HALO + own_rows] = owns[c]
        ext[c, HALO + own_rows :] = after[c]
    rows, lanes = ext.shape[1], ext.shape[2]
    lane = lax.broadcasted_iota(jnp.int32, (rows, lanes), 1)
    top = lane == lanes - 1
    bottom = lane == 0

    def east(x):
        return pltpu.roll(x, rows - 1, 0)

    def west(x):
        return pltpu.roll(x, 1, 0)

    def up(x):
        return pltpu.roll(x, lanes - 1, 1)

    def down(x):
        return pltpu.roll(x, 1, 1)

    depth, rotation, cell, east_len, north_len = (ext[c] for c in range(3, CHANNELS))
    wave_x = jnp.sqrt(jnp.maximum(depth, east(depth)))
    depth_e = east(depth)
    depth_up = jnp.where(top, depth, up(depth))
    wave_y = jnp.sqrt(jnp.maximum(depth, depth_up))
    root_d = jnp.sqrt(depth)
    factor = time_step / cell
    height, speed_x, speed_y = ext[0], ext[1], ext[2]
    for number in range(STEPS):
        h_e, u_e, v_e = east(height), east(speed_x), east(speed_y)
        flux_h = east_len * (
            0.5 * (depth * speed_x + depth_e * u_e) - 0.5 * wave_x * (h_e - height)
        )
        flux_u = east_len * (0.5 * (height + h_e) - 0.5 * wave_x * (u_e - speed_x))
        flux_v = east_len * (-0.5 * wave_x * (v_e - speed_y))
        h_up = jnp.where(top, height, up(height))
        u_up = jnp.where(top, speed_x, up(speed_x))
        v_up = jnp.where(top, -speed_y, up(speed_y))
        north_h = north_len * (
            0.5 * (depth * speed_y + depth_up * v_up) - 0.5 * wave_y * (h_up - height)
        )
        north_u = north_len * (-0.5 * wave_y * (u_up - speed_x))
        north_v = north_len * (0.5 * (height + h_up) - 0.5 * wave_y * (v_up - speed_y))
        wall_v = north_len * (height - root_d * speed_y)
        south_h = jnp.where(bottom, 0.0, down(north_h))
        south_u = jnp.where(bottom, 0.0, down(north_u))
        south_v = jnp.where(bottom, wall_v, down(north_v))
        new_h = height - factor * (flux_h - west(flux_h) + north_h - south_h)
        new_u = (
            speed_x
            - factor * (flux_u - west(flux_u) + north_u - south_u)
            + time_step * rotation * speed_y
        )
        new_v = (
            speed_y
            - factor * (flux_v - west(flux_v) + north_v - south_v)
            - time_step * rotation * speed_x
        )
        height, speed_x, speed_y = new_h, new_u, new_v
        snap_ref[number] = height[HALO : HALO + own_rows].astype(snap_ref.dtype)
    final_ref[0] = height[HALO : HALO + own_rows]
    final_ref[1] = speed_x[HALO : HALO + own_rows]
    final_ref[2] = speed_y[HALO : HALO + own_rows]


def stencil(initial, depth_field, coriolis, cell_area, face_len, before, after):
    rows, lanes = depth_field.shape
    whole = lambda shape: pl.BlockSpec(shape, lambda: (0,) * len(shape))
    return pl.pallas_call(
        stencil_kernel,
        out_shape=(
            jax.ShapeDtypeStruct((3, rows, lanes), jnp.float32),
            jax.ShapeDtypeStruct((STEPS, rows, lanes), jnp.bfloat16),
        ),
        in_specs=[
            whole(initial.shape), whole(depth_field.shape), whole(coriolis.shape),
            whole(cell_area.shape), whole(face_len.shape), whole(before.shape), whole(after.shape),
        ],
        out_specs=(whole((3, rows, lanes)), whole((STEPS, rows, lanes))),
        scratch_shapes=[pltpu.VMEM((CHANNELS, rows + 2 * HALO, lanes), jnp.float32)],
    )(initial, depth_field, coriolis, cell_area, face_len, before, after)


def halo_exchange(near, far, axis):
    count = lax.axis_size(axis)
    odd = lax.axis_index(axis) % 2 == 1
    near_in = lax.ppermute(near, axis, [(i, i ^ 1) for i in range(count)])
    far_in = lax.ppermute(
        far, axis, [(i, (i + 1) % count if i % 2 else (i - 1) % count) for i in range(count)]
    )
    return jnp.where(odd, near_in, far_in), jnp.where(odd, far_in, near_in)


def on_device(initial, depth_field, coriolis, cell_area, face_len, owners, offsets, weights):
    odd = (lax.axis_index("tile") % 2).astype(jnp.int32).reshape(1)
    near, far = edges(odd, initial, depth_field, coriolis, cell_area, face_len)
    before, after = halo_exchange(near, far, "tile")
    fields, snaps = stencil(initial, depth_field, coriolis, cell_area, face_len, before, after)
    snapped = snaps.reshape(STEPS, -1, 128)
    contribution = jnp.einsum(
        "sbk,brkt->brst", snapped, weights, preferred_element_type=jnp.float32
    )
    slot_count = weights.shape[0] * weights.shape[1]
    flat = contribution.reshape(slot_count, STEPS * 128)
    n_tile = lax.axis_size("tile")
    item = jnp.arange(slot_count, dtype=jnp.int32)
    own_owner = owners.reshape(-1)
    same = own_owner[:, None] == own_owner[None, :]
    rank = jnp.sum((same & (item[None, :] < item[:, None])).astype(jnp.int32), axis=1)
    slot = own_owner * CAP + rank
    pack = (jnp.arange(n_tile * CAP, dtype=jnp.int32)[:, None] == slot[None, :]).astype(
        jnp.float32
    )
    send = jnp.dot(pack, flat, precision=lax.Precision.HIGHEST, preferred_element_type=jnp.float32)
    labels = jnp.dot(
        pack,
        offsets.reshape(-1, 1).astype(jnp.float32) + 1.0,
        precision=lax.Precision.HIGHEST,
        preferred_element_type=jnp.float32,
    ).reshape(n_tile, CAP) - 1.0
    label_row = jnp.pad(labels, ((0, 0), (0, 128 - CAP)))
    payload = jnp.concatenate([send.reshape(n_tile, CAP * STEPS * 128), label_row], axis=1)
    recv = lax.all_to_all(payload, "tile", 0, 0, tiled=True)
    recv_data = recv[:, : CAP * STEPS * 128].reshape(n_tile * CAP, STEPS * 128)
    recv_offset = recv[:, CAP * STEPS * 128 : CAP * STEPS * 128 + CAP].reshape(-1)
    unpack = (
        recv_offset[None, :] == jnp.arange(TB, dtype=jnp.float32)[:, None]
    ).astype(jnp.float32)
    gathered = jnp.dot(
        unpack, recv_data, precision=lax.Precision.HIGHEST, preferred_element_type=jnp.float32
    )
    return (gathered.reshape(TB, STEPS, 128), fields)


def solution(mesh):
    placed = (
        P(None, ("exp", "tile"), None),
        P(("exp", "tile"), None),
        P(("exp", "tile"), None),
        P(("exp", "tile"), None),
        P(None, ("exp", "tile"), None),
        P(("exp", "tile"), None),
        P(("exp", "tile"), None),
        P(("exp", "tile"), None, None, None),
    )
    return jax.shard_map(
        on_device,
        mesh=mesh,
        in_specs=placed,
        out_specs=(P(("exp", "tile"), None, None), P(None, ("exp", "tile"), None)),
        check_vma=False,
    )
```

```python
import jax
import jax.numpy as jnp
from jax import lax
from jax.sharding import PartitionSpec as P
from jax.experimental import pallas as pl
from jax.experimental.pallas import tpu as pltpu

STEPS = 4
TB = 16
CAP = 4
HALO = 8
CHANNELS = 8


time_step = 0.3


def with_halo(cells, sides, width):
    for axis, dim in sides:
        count = lax.axis_size(axis)
        head = lax.slice_in_dim(cells, 0, width, axis=dim)
        tail = lax.slice_in_dim(cells, cells.shape[dim] - width, cells.shape[dim], axis=dim)
        if count % 2 == 0:
            odd = lax.axis_index(axis) % 2 == 1
            near = lax.ppermute(
                jnp.where(odd, head, tail), axis, [(i, i ^ 1) for i in range(count)]
            )
            far = lax.ppermute(
                jnp.where(odd, tail, head),
                axis,
                [(i, (i + 1) % count if i % 2 else (i - 1) % count) for i in range(count)],
            )
            before = jnp.where(odd, near, far)
            after = jnp.where(odd, far, near)
        else:
            before = lax.ppermute(tail, axis, [(i, (i + 1) % count) for i in range(count)])
            after = lax.ppermute(head, axis, [((i + 1) % count, i) for i in range(count)])
        cells = jnp.concatenate([before, cells, after], axis=dim)
    return cells


def advance(fields, metric):
    height, speed_x, speed_y = (fields[0], fields[1], fields[2])
    depth, rotation, area, east_len, north_len = (
        metric[0],
        metric[1],
        metric[2],
        metric[3],
        metric[4],
    )
    wave_x = jnp.sqrt(jnp.maximum(depth[:-1], depth[1:]))
    edge = east_len[:-1]
    flux_h = edge * (
        0.5 * (depth[:-1] * speed_x[:-1] + depth[1:] * speed_x[1:])
        - 0.5 * wave_x * (height[1:] - height[:-1])
    )
    flux_u = edge * (0.5 * (height[:-1] + height[1:]) - 0.5 * wave_x * (speed_x[1:] - speed_x[:-1]))
    flux_v = edge * (-0.5 * wave_x * (speed_y[1:] - speed_y[:-1]))
    own_h = height[1:-1]
    own_u = speed_x[1:-1]
    own_v = speed_y[1:-1]
    own_d = depth[1:-1]
    own_f = rotation[1:-1]
    own_a = area[1:-1]
    own_n = north_len[1:-1]
    above_h = jnp.concatenate([own_h[:, 1:], own_h[:, -1:]], axis=1)
    above_u = jnp.concatenate([own_u[:, 1:], own_u[:, -1:]], axis=1)
    above_v = jnp.concatenate([own_v[:, 1:], -own_v[:, -1:]], axis=1)
    above_d = jnp.concatenate([own_d[:, 1:], own_d[:, -1:]], axis=1)
    wave_y = jnp.sqrt(jnp.maximum(own_d, above_d))
    north_h = own_n * (0.5 * (own_d * own_v + above_d * above_v) - 0.5 * wave_y * (above_h - own_h))
    north_u = own_n * (-0.5 * wave_y * (above_u - own_u))
    north_v = own_n * (0.5 * (own_h + above_h) - 0.5 * wave_y * (above_v - own_v))
    wall_v = own_n[:, :1] * (own_h[:, :1] - jnp.sqrt(own_d[:, :1]) * own_v[:, :1])
    zeros = jnp.zeros_like(wall_v)
    south_h = jnp.concatenate([zeros, north_h[:, :-1]], axis=1)
    south_u = jnp.concatenate([zeros, north_u[:, :-1]], axis=1)
    south_v = jnp.concatenate([wall_v, north_v[:, :-1]], axis=1)
    factor = time_step / own_a
    new_h = own_h - factor * (flux_h[1:] - flux_h[:-1] + north_h - south_h)
    new_u = (
        own_u - factor * (flux_u[1:] - flux_u[:-1] + north_u - south_u) + time_step * own_f * own_v
    )
    new_v = (
        own_v - factor * (flux_v[1:] - flux_v[:-1] + north_v - south_v) - time_step * own_f * own_u
    )
    return jnp.stack([new_h, new_u, new_v])


def edge_kernel(odd_ref, ini_h, ini_t, dep_h, dep_t, cor_h, cor_t, area_h, area_t, face_h, face_t, near_ref, far_ref):
    odd = odd_ref[0] == 1
    head = [ini_h[0], ini_h[1], ini_h[2], dep_h[...], cor_h[...], area_h[...], face_h[0], face_h[1]]
    tail = [ini_t[0], ini_t[1], ini_t[2], dep_t[...], cor_t[...], area_t[...], face_t[0], face_t[1]]
    for c in range(CHANNELS):
        near_ref[c] = jnp.where(odd, head[c], tail[c])
        far_ref[c] = jnp.where(odd, tail[c], head[c])


def edges(odd, initial, depth_field, coriolis, cell_area, face_len):
    rows, lanes = depth_field.shape
    last = rows // HALO - 1
    spec3 = lambda b: pl.BlockSpec((3, HALO, lanes), lambda i: (0, b, 0))
    spec2 = lambda b: pl.BlockSpec((HALO, lanes), lambda i: (b, 0))
    specf = lambda b: pl.BlockSpec((2, HALO, lanes), lambda i: (0, b, 0))
    out = jax.ShapeDtypeStruct((CHANNELS, HALO, lanes), jnp.float32)
    return pl.pallas_call(
        edge_kernel,
        out_shape=(out, out),
        in_specs=[
            pl.BlockSpec(memory_space=pltpu.SMEM),
            spec3(0), spec3(last), spec2(0), spec2(last), spec2(0), spec2(last),
            spec2(0), spec2(last), specf(0), specf(last),
        ],
        out_specs=(
            pl.BlockSpec((CHANNELS, HALO, lanes), lambda i: (0, 0, 0)),
            pl.BlockSpec((CHANNELS, HALO, lanes), lambda i: (0, 0, 0)),
        ),
        grid=(1,),
    )(odd, initial, initial, depth_field, depth_field, coriolis, coriolis, cell_area, cell_area, face_len, face_len)


def stencil_kernel(odd_ref, ini, dep, cor, area, face, near_in, far_in, final_ref, snap_ref, ext):
    own_rows = ini.shape[1]
    odd = odd_ref[0] == 1
    owns = [ini[0], ini[1], ini[2], dep[...], cor[...], area[...], face[0], face[1]]
    for c in range(CHANNELS):
        ext[c, :HALO] = jnp.where(odd, near_in[c], far_in[c])
        ext[c, HALO : HALO + own_rows] = owns[c]
        ext[c, HALO + own_rows :] = jnp.where(odd, far_in[c], near_in[c])
    rows, lanes = ext.shape[1], ext.shape[2]
    lane = lax.broadcasted_iota(jnp.int32, (rows, lanes), 1)
    top = lane == lanes - 1
    bottom = lane == 0

    def east(x):
        return pltpu.roll(x, rows - 1, 0)

    def west(x):
        return pltpu.roll(x, 1, 0)

    def up(x):
        return pltpu.roll(x, lanes - 1, 1)

    def down(x):
        return pltpu.roll(x, 1, 1)

    depth, rotation, cell, east_len, north_len = (ext[c] for c in range(3, CHANNELS))
    wave_x = jnp.sqrt(jnp.maximum(depth, east(depth)))
    depth_e = east(depth)
    depth_up = jnp.where(top, depth, up(depth))
    wave_y = jnp.sqrt(jnp.maximum(depth, depth_up))
    root_d = jnp.sqrt(depth)
    factor = time_step / cell
    height, speed_x, speed_y = ext[0], ext[1], ext[2]
    for number in range(STEPS):
        h_e, u_e, v_e = east(height), east(speed_x), east(speed_y)
        flux_h = east_len * (
            0.5 * (depth * speed_x + depth_e * u_e) - 0.5 * wave_x * (h_e - height)
        )
        flux_u = east_len * (0.5 * (height + h_e) - 0.5 * wave_x * (u_e - speed_x))
        flux_v = east_len * (-0.5 * wave_x * (v_e - speed_y))
        h_up = jnp.where(top, height, up(height))
        u_up = jnp.where(top, speed_x, up(speed_x))
        v_up = jnp.where(top, -speed_y, up(speed_y))
        north_h = north_len * (
            0.5 * (depth * speed_y + depth_up * v_up) - 0.5 * wave_y * (h_up - height)
        )
        north_u = north_len * (-0.5 * wave_y * (u_up - speed_x))
        north_v = north_len * (0.5 * (height + h_up) - 0.5 * wave_y * (v_up - speed_y))
        wall_v = north_len * (height - root_d * speed_y)
        south_h = jnp.where(bottom, 0.0, down(north_h))
        south_u = jnp.where(bottom, 0.0, down(north_u))
        south_v = jnp.where(bottom, wall_v, down(north_v))
        new_h = height - factor * (flux_h - west(flux_h) + north_h - south_h)
        new_u = (
            speed_x
            - factor * (flux_u - west(flux_u) + north_u - south_u)
            + time_step * rotation * speed_y
        )
        new_v = (
            speed_y
            - factor * (flux_v - west(flux_v) + north_v - south_v)
            - time_step * rotation * speed_x
        )
        height, speed_x, speed_y = new_h, new_u, new_v
        for half in range(lanes // 128):
            snap_ref[number, half] = height[
                HALO : HALO + own_rows, half * 128 : (half + 1) * 128
            ].astype(snap_ref.dtype)
    final_ref[0] = height[HALO : HALO + own_rows]
    final_ref[1] = speed_x[HALO : HALO + own_rows]
    final_ref[2] = speed_y[HALO : HALO + own_rows]


def stencil(odd, initial, depth_field, coriolis, cell_area, face_len, near_in, far_in):
    rows, lanes = depth_field.shape
    whole = lambda shape: pl.BlockSpec(shape, lambda: (0,) * len(shape))
    snap_shape = (STEPS, lanes // 128, rows, 128)
    return pl.pallas_call(
        stencil_kernel,
        out_shape=(
            jax.ShapeDtypeStruct((3, rows, lanes), jnp.float32),
            jax.ShapeDtypeStruct(snap_shape, jnp.bfloat16),
        ),
        in_specs=[
            pl.BlockSpec(memory_space=pltpu.SMEM),
            whole(initial.shape), whole(depth_field.shape), whole(coriolis.shape),
            whole(cell_area.shape), whole(face_len.shape), whole(near_in.shape), whole(far_in.shape),
        ],
        out_specs=(whole((3, rows, lanes)), whole(snap_shape)),
        scratch_shapes=[pltpu.VMEM((CHANNELS, rows + 2 * HALO, lanes), jnp.float32)],
    )(odd, initial, depth_field, coriolis, cell_area, face_len, near_in, far_in)


def halo_exchange(near, far, axis):
    count = lax.axis_size(axis)
    odd = lax.axis_index(axis) % 2 == 1
    near_in = lax.ppermute(near, axis, [(i, i ^ 1) for i in range(count)])
    far_in = lax.ppermute(
        far, axis, [(i, (i + 1) % count if i % 2 else (i - 1) % count) for i in range(count)]
    )
    return near_in, far_in


def on_device(initial, depth_field, coriolis, cell_area, face_len, owners, offsets, weights):
    odd = (lax.axis_index("tile") % 2).astype(jnp.int32).reshape(1)
    near, far = edges(odd, initial, depth_field, coriolis, cell_area, face_len)
    near_in, far_in = halo_exchange(near, far, "tile")
    fields, snaps = stencil(odd, initial, depth_field, coriolis, cell_area, face_len, near_in, far_in)
    halves = snaps.shape[1]
    grouped = weights.reshape((-1, halves) + weights.shape[1:])
    contribution = jnp.einsum(
        "shck,chrkt->chrst", snaps, grouped, preferred_element_type=jnp.float32
    )
    slot_count = weights.shape[0] * weights.shape[1]
    flat = contribution.reshape(slot_count, STEPS * 128)
    n_tile = lax.axis_size("tile")
    item = jnp.arange(slot_count, dtype=jnp.int32)
    own_owner = owners.reshape(-1)
    same = own_owner[:, None] == own_owner[None, :]
    rank = jnp.sum((same & (item[None, :] < item[:, None])).astype(jnp.int32), axis=1)
    slot = own_owner * CAP + rank
    pack = (jnp.arange(n_tile * CAP, dtype=jnp.int32)[:, None] == slot[None, :]).astype(
        jnp.float32
    )
    send = jnp.dot(pack, flat, precision=lax.Precision.HIGHEST, preferred_element_type=jnp.float32)
    labels = jnp.dot(
        pack,
        offsets.reshape(-1, 1).astype(jnp.float32) + 1.0,
        precision=lax.Precision.HIGHEST,
        preferred_element_type=jnp.float32,
    ).reshape(n_tile, CAP) - 1.0
    label_row = jnp.pad(labels, ((0, 0), (0, 128 - CAP)))
    payload = jnp.concatenate([send.reshape(n_tile, CAP * STEPS * 128), label_row], axis=1)
    recv = lax.all_to_all(payload, "tile", 0, 0, tiled=True)
    recv_data = recv[:, : CAP * STEPS * 128].reshape(n_tile * CAP, STEPS * 128)
    recv_offset = recv[:, CAP * STEPS * 128 : CAP * STEPS * 128 + CAP].reshape(-1)
    unpack = (
        recv_offset[None, :] == jnp.arange(TB, dtype=jnp.float32)[:, None]
    ).astype(jnp.float32)
    gathered = jnp.einsum(
        "tq,qsk->tsk",
        unpack,
        recv_data.reshape(n_tile * CAP, STEPS, 128),
        precision=lax.Precision.HIGHEST,
        preferred_element_type=jnp.float32,
    )
    return (gathered, fields)


def solution(mesh):
    placed = (
        P(None, ("exp", "tile"), None),
        P(("exp", "tile"), None),
        P(("exp", "tile"), None),
        P(("exp", "tile"), None),
        P(None, ("exp", "tile"), None),
        P(("exp", "tile"), None),
        P(("exp", "tile"), None),
        P(("exp", "tile"), None, None, None),
    )
    return jax.shard_map(
        on_device,
        mesh=mesh,
        in_specs=placed,
        out_specs=(P(("exp", "tile"), None, None), P(None, ("exp", "tile"), None)),
        check_vma=False,
    )
```

```python
import jax
import jax.numpy as jnp
from jax import lax
from jax.sharding import PartitionSpec as P
from jax.experimental import pallas as pl
from jax.experimental.pallas import tpu as pltpu

STEPS = 4
TB = 16
CAP = 4
HALO = 8
CHANNELS = 8


time_step = 0.3


def with_halo(cells, sides, width):
    for axis, dim in sides:
        count = lax.axis_size(axis)
        head = lax.slice_in_dim(cells, 0, width, axis=dim)
        tail = lax.slice_in_dim(cells, cells.shape[dim] - width, cells.shape[dim], axis=dim)
        if count % 2 == 0:
            odd = lax.axis_index(axis) % 2 == 1
            near = lax.ppermute(
                jnp.where(odd, head, tail), axis, [(i, i ^ 1) for i in range(count)]
            )
            far = lax.ppermute(
                jnp.where(odd, tail, head),
                axis,
                [(i, (i + 1) % count if i % 2 else (i - 1) % count) for i in range(count)],
            )
            before = jnp.where(odd, near, far)
            after = jnp.where(odd, far, near)
        else:
            before = lax.ppermute(tail, axis, [(i, (i + 1) % count) for i in range(count)])
            after = lax.ppermute(head, axis, [((i + 1) % count, i) for i in range(count)])
        cells = jnp.concatenate([before, cells, after], axis=dim)
    return cells


def advance(fields, metric):
    height, speed_x, speed_y = (fields[0], fields[1], fields[2])
    depth, rotation, area, east_len, north_len = (
        metric[0],
        metric[1],
        metric[2],
        metric[3],
        metric[4],
    )
    wave_x = jnp.sqrt(jnp.maximum(depth[:-1], depth[1:]))
    edge = east_len[:-1]
    flux_h = edge * (
        0.5 * (depth[:-1] * speed_x[:-1] + depth[1:] * speed_x[1:])
        - 0.5 * wave_x * (height[1:] - height[:-1])
    )
    flux_u = edge * (0.5 * (height[:-1] + height[1:]) - 0.5 * wave_x * (speed_x[1:] - speed_x[:-1]))
    flux_v = edge * (-0.5 * wave_x * (speed_y[1:] - speed_y[:-1]))
    own_h = height[1:-1]
    own_u = speed_x[1:-1]
    own_v = speed_y[1:-1]
    own_d = depth[1:-1]
    own_f = rotation[1:-1]
    own_a = area[1:-1]
    own_n = north_len[1:-1]
    above_h = jnp.concatenate([own_h[:, 1:], own_h[:, -1:]], axis=1)
    above_u = jnp.concatenate([own_u[:, 1:], own_u[:, -1:]], axis=1)
    above_v = jnp.concatenate([own_v[:, 1:], -own_v[:, -1:]], axis=1)
    above_d = jnp.concatenate([own_d[:, 1:], own_d[:, -1:]], axis=1)
    wave_y = jnp.sqrt(jnp.maximum(own_d, above_d))
    north_h = own_n * (0.5 * (own_d * own_v + above_d * above_v) - 0.5 * wave_y * (above_h - own_h))
    north_u = own_n * (-0.5 * wave_y * (above_u - own_u))
    north_v = own_n * (0.5 * (own_h + above_h) - 0.5 * wave_y * (above_v - own_v))
    wall_v = own_n[:, :1] * (own_h[:, :1] - jnp.sqrt(own_d[:, :1]) * own_v[:, :1])
    zeros = jnp.zeros_like(wall_v)
    south_h = jnp.concatenate([zeros, north_h[:, :-1]], axis=1)
    south_u = jnp.concatenate([zeros, north_u[:, :-1]], axis=1)
    south_v = jnp.concatenate([wall_v, north_v[:, :-1]], axis=1)
    factor = time_step / own_a
    new_h = own_h - factor * (flux_h[1:] - flux_h[:-1] + north_h - south_h)
    new_u = (
        own_u - factor * (flux_u[1:] - flux_u[:-1] + north_u - south_u) + time_step * own_f * own_v
    )
    new_v = (
        own_v - factor * (flux_v[1:] - flux_v[:-1] + north_v - south_v) - time_step * own_f * own_u
    )
    return jnp.stack([new_h, new_u, new_v])


def edge_kernel(odd_ref, ini_h, ini_t, dep_h, dep_t, cor_h, cor_t, area_h, area_t, face_h, face_t, near_ref, far_ref):
    odd = odd_ref[0] == 1
    head = [ini_h[0], ini_h[1], ini_h[2], dep_h[...], cor_h[...], area_h[...], face_h[0], face_h[1]]
    tail = [ini_t[0], ini_t[1], ini_t[2], dep_t[...], cor_t[...], area_t[...], face_t[0], face_t[1]]
    for c in range(CHANNELS):
        near_ref[c] = jnp.where(odd, head[c], tail[c])
        far_ref[c] = jnp.where(odd, tail[c], head[c])


def edges(odd, initial, depth_field, coriolis, cell_area, face_len):
    rows, lanes = depth_field.shape
    last = rows // HALO - 1
    spec3 = lambda b: pl.BlockSpec((3, HALO, lanes), lambda i: (0, b, 0))
    spec2 = lambda b: pl.BlockSpec((HALO, lanes), lambda i: (b, 0))
    specf = lambda b: pl.BlockSpec((2, HALO, lanes), lambda i: (0, b, 0))
    out = jax.ShapeDtypeStruct((CHANNELS, HALO, lanes), jnp.float32)
    return pl.pallas_call(
        edge_kernel,
        out_shape=(out, out),
        in_specs=[
            pl.BlockSpec(memory_space=pltpu.SMEM),
            spec3(0), spec3(last), spec2(0), spec2(last), spec2(0), spec2(last),
            spec2(0), spec2(last), specf(0), specf(last),
        ],
        out_specs=(
            pl.BlockSpec((CHANNELS, HALO, lanes), lambda i: (0, 0, 0)),
            pl.BlockSpec((CHANNELS, HALO, lanes), lambda i: (0, 0, 0)),
        ),
        grid=(1,),
    )(odd, initial, initial, depth_field, depth_field, coriolis, coriolis, cell_area, cell_area, face_len, face_len)


def stencil_kernel(odd_ref, ini, dep, cor, area, face, near_in, far_in, final_ref, snap_ref, ext):
    own_rows = ini.shape[1]
    odd = odd_ref[0] == 1
    owns = [ini[0], ini[1], ini[2], dep[...], cor[...], area[...], face[0], face[1]]
    for c in range(CHANNELS):
        ext[c, :HALO] = jnp.where(odd, near_in[c], far_in[c])
        ext[c, HALO : HALO + own_rows] = owns[c]
        ext[c, HALO + own_rows :] = jnp.where(odd, far_in[c], near_in[c])
    rows, lanes = ext.shape[1], ext.shape[2]
    lane = lax.broadcasted_iota(jnp.int32, (rows, lanes), 1)
    top = lane == lanes - 1
    bottom = lane == 0

    def east(x):
        return pltpu.roll(x, rows - 1, 0)

    def west(x):
        return pltpu.roll(x, 1, 0)

    def up(x):
        return pltpu.roll(x, lanes - 1, 1)

    def down(x):
        return pltpu.roll(x, 1, 1)

    depth, rotation, cell, east_len, north_len = (ext[c] for c in range(3, CHANNELS))
    wave_x = jnp.sqrt(jnp.maximum(depth, east(depth)))
    depth_e = east(depth)
    depth_up = jnp.where(top, depth, up(depth))
    wave_y = jnp.sqrt(jnp.maximum(depth, depth_up))
    root_d = jnp.sqrt(depth)
    factor = time_step / cell
    height, speed_x, speed_y = ext[0], ext[1], ext[2]
    for number in range(STEPS):
        h_e, u_e, v_e = east(height), east(speed_x), east(speed_y)
        flux_h = east_len * (
            0.5 * (depth * speed_x + depth_e * u_e) - 0.5 * wave_x * (h_e - height)
        )
        flux_u = east_len * (0.5 * (height + h_e) - 0.5 * wave_x * (u_e - speed_x))
        flux_v = east_len * (-0.5 * wave_x * (v_e - speed_y))
        h_up = jnp.where(top, height, up(height))
        u_up = jnp.where(top, speed_x, up(speed_x))
        v_up = jnp.where(top, -speed_y, up(speed_y))
        north_h = north_len * (
            0.5 * (depth * speed_y + depth_up * v_up) - 0.5 * wave_y * (h_up - height)
        )
        north_u = north_len * (-0.5 * wave_y * (u_up - speed_x))
        north_v = north_len * (0.5 * (height + h_up) - 0.5 * wave_y * (v_up - speed_y))
        wall_v = north_len * (height - root_d * speed_y)
        south_h = jnp.where(bottom, 0.0, down(north_h))
        south_u = jnp.where(bottom, 0.0, down(north_u))
        south_v = jnp.where(bottom, wall_v, down(north_v))
        new_h = height - factor * (flux_h - west(flux_h) + north_h - south_h)
        new_u = (
            speed_x
            - factor * (flux_u - west(flux_u) + north_u - south_u)
            + time_step * rotation * speed_y
        )
        new_v = (
            speed_y
            - factor * (flux_v - west(flux_v) + north_v - south_v)
            - time_step * rotation * speed_x
        )
        height, speed_x, speed_y = new_h, new_u, new_v
        for half in range(lanes // 128):
            snap_ref[number, half] = height[
                HALO : HALO + own_rows, half * 128 : (half + 1) * 128
            ].astype(snap_ref.dtype)
    final_ref[0] = height[HALO : HALO + own_rows]
    final_ref[1] = speed_x[HALO : HALO + own_rows]
    final_ref[2] = speed_y[HALO : HALO + own_rows]


def stencil(odd, initial, depth_field, coriolis, cell_area, face_len, near_in, far_in):
    rows, lanes = depth_field.shape
    whole = lambda shape: pl.BlockSpec(shape, lambda: (0,) * len(shape))
    snap_shape = (STEPS, lanes // 128, rows, 128)
    return pl.pallas_call(
        stencil_kernel,
        out_shape=(
            jax.ShapeDtypeStruct((3, rows, lanes), jnp.float32),
            jax.ShapeDtypeStruct(snap_shape, jnp.bfloat16),
        ),
        in_specs=[
            pl.BlockSpec(memory_space=pltpu.SMEM),
            whole(initial.shape), whole(depth_field.shape), whole(coriolis.shape),
            whole(cell_area.shape), whole(face_len.shape), whole(near_in.shape), whole(far_in.shape),
        ],
        out_specs=(whole((3, rows, lanes)), whole(snap_shape)),
        scratch_shapes=[pltpu.VMEM((CHANNELS, rows + 2 * HALO, lanes), jnp.float32)],
    )(odd, initial, depth_field, coriolis, cell_area, face_len, near_in, far_in)


def halo_exchange(near, far, axis):
    count = lax.axis_size(axis)
    odd = lax.axis_index(axis) % 2 == 1
    near_in = lax.ppermute(near, axis, [(i, i ^ 1) for i in range(count)])
    far_in = lax.ppermute(
        far, axis, [(i, (i + 1) % count if i % 2 else (i - 1) % count) for i in range(count)]
    )
    return near_in, far_in


def on_device(initial, depth_field, coriolis, cell_area, face_len, owners, offsets, weights):
    odd = (lax.axis_index("tile") % 2).astype(jnp.int32).reshape(1)
    near, far = edges(odd, initial, depth_field, coriolis, cell_area, face_len)
    near_in, far_in = halo_exchange(near, far, "tile")
    halves = initial.shape[2] // 128
    grouped = weights.reshape((-1, halves) + weights.shape[1:])
    columns = initial.shape[1]
    lo, hi = STEPS, columns - STEPS

    def contribute(snaps, first, last):
        return jnp.einsum(
            "shck,chrkt->chrst",
            snaps[:, :, first:last],
            grouped[first:last],
            preferred_element_type=jnp.float32,
        )

    _, inner_snaps = stencil(odd, initial, depth_field, coriolis, cell_area, face_len, near, far)
    inner = contribute(inner_snaps, lo, hi)
    fields, snaps = stencil(odd, initial, depth_field, coriolis, cell_area, face_len, near_in, far_in)
    contribution = jnp.concatenate(
        [contribute(snaps, 0, lo), inner, contribute(snaps, hi, columns)], axis=0
    )
    slot_count = weights.shape[0] * weights.shape[1]
    flat = contribution.reshape(slot_count, STEPS * 128)
    n_tile = lax.axis_size("tile")
    item = jnp.arange(slot_count, dtype=jnp.int32)
    own_owner = owners.reshape(-1)
    same = own_owner[:, None] == own_owner[None, :]
    rank = jnp.sum((same & (item[None, :] < item[:, None])).astype(jnp.int32), axis=1)
    slot = own_owner * CAP + rank
    pack = (jnp.arange(n_tile * CAP, dtype=jnp.int32)[:, None] == slot[None, :]).astype(
        jnp.float32
    )
    send = jnp.dot(pack, flat, precision=lax.Precision.HIGHEST, preferred_element_type=jnp.float32)
    labels = jnp.dot(
        pack,
        offsets.reshape(-1, 1).astype(jnp.float32) + 1.0,
        precision=lax.Precision.HIGHEST,
        preferred_element_type=jnp.float32,
    ).reshape(n_tile, CAP) - 1.0
    label_row = jnp.pad(labels, ((0, 0), (0, 128 - CAP)))
    payload = jnp.concatenate([send.reshape(n_tile, CAP * STEPS * 128), label_row], axis=1)
    recv = lax.all_to_all(payload, "tile", 0, 0, tiled=True)
    recv_data = recv[:, : CAP * STEPS * 128].reshape(n_tile * CAP, STEPS * 128)
    recv_offset = recv[:, CAP * STEPS * 128 : CAP * STEPS * 128 + CAP].reshape(-1)
    unpack = (
        recv_offset[None, :] == jnp.arange(TB, dtype=jnp.float32)[:, None]
    ).astype(jnp.float32)
    gathered = jnp.einsum(
        "tq,qsk->tsk",
        unpack,
        recv_data.reshape(n_tile * CAP, STEPS, 128),
        precision=lax.Precision.HIGHEST,
        preferred_element_type=jnp.float32,
    )
    return (gathered, fields)


def solution(mesh):
    placed = (
        P(None, ("exp", "tile"), None),
        P(("exp", "tile"), None),
        P(("exp", "tile"), None),
        P(("exp", "tile"), None),
        P(None, ("exp", "tile"), None),
        P(("exp", "tile"), None),
        P(("exp", "tile"), None),
        P(("exp", "tile"), None, None, None),
    )
    return jax.shard_map(
        on_device,
        mesh=mesh,
        in_specs=placed,
        out_specs=(P(("exp", "tile"), None, None), P(None, ("exp", "tile"), None)),
        check_vma=False,
    )
```

```python
import jax
import jax.numpy as jnp
from jax import lax
from jax.sharding import PartitionSpec as P
from jax.experimental import pallas as pl
from jax.experimental.pallas import tpu as pltpu

STEPS = 4
TB = 16
CAP = 4
HALO = 8
CHANNELS = 8


time_step = 0.3


def with_halo(cells, sides, width):
    for axis, dim in sides:
        count = lax.axis_size(axis)
        head = lax.slice_in_dim(cells, 0, width, axis=dim)
        tail = lax.slice_in_dim(cells, cells.shape[dim] - width, cells.shape[dim], axis=dim)
        if count % 2 == 0:
            odd = lax.axis_index(axis) % 2 == 1
            near = lax.ppermute(
                jnp.where(odd, head, tail), axis, [(i, i ^ 1) for i in range(count)]
            )
            far = lax.ppermute(
                jnp.where(odd, tail, head),
                axis,
                [(i, (i + 1) % count if i % 2 else (i - 1) % count) for i in range(count)],
            )
            before = jnp.where(odd, near, far)
            after = jnp.where(odd, far, near)
        else:
            before = lax.ppermute(tail, axis, [(i, (i + 1) % count) for i in range(count)])
            after = lax.ppermute(head, axis, [((i + 1) % count, i) for i in range(count)])
        cells = jnp.concatenate([before, cells, after], axis=dim)
    return cells


def advance(fields, metric):
    height, speed_x, speed_y = (fields[0], fields[1], fields[2])
    depth, rotation, area, east_len, north_len = (
        metric[0],
        metric[1],
        metric[2],
        metric[3],
        metric[4],
    )
    wave_x = jnp.sqrt(jnp.maximum(depth[:-1], depth[1:]))
    edge = east_len[:-1]
    flux_h = edge * (
        0.5 * (depth[:-1] * speed_x[:-1] + depth[1:] * speed_x[1:])
        - 0.5 * wave_x * (height[1:] - height[:-1])
    )
    flux_u = edge * (0.5 * (height[:-1] + height[1:]) - 0.5 * wave_x * (speed_x[1:] - speed_x[:-1]))
    flux_v = edge * (-0.5 * wave_x * (speed_y[1:] - speed_y[:-1]))
    own_h = height[1:-1]
    own_u = speed_x[1:-1]
    own_v = speed_y[1:-1]
    own_d = depth[1:-1]
    own_f = rotation[1:-1]
    own_a = area[1:-1]
    own_n = north_len[1:-1]
    above_h = jnp.concatenate([own_h[:, 1:], own_h[:, -1:]], axis=1)
    above_u = jnp.concatenate([own_u[:, 1:], own_u[:, -1:]], axis=1)
    above_v = jnp.concatenate([own_v[:, 1:], -own_v[:, -1:]], axis=1)
    above_d = jnp.concatenate([own_d[:, 1:], own_d[:, -1:]], axis=1)
    wave_y = jnp.sqrt(jnp.maximum(own_d, above_d))
    north_h = own_n * (0.5 * (own_d * own_v + above_d * above_v) - 0.5 * wave_y * (above_h - own_h))
    north_u = own_n * (-0.5 * wave_y * (above_u - own_u))
    north_v = own_n * (0.5 * (own_h + above_h) - 0.5 * wave_y * (above_v - own_v))
    wall_v = own_n[:, :1] * (own_h[:, :1] - jnp.sqrt(own_d[:, :1]) * own_v[:, :1])
    zeros = jnp.zeros_like(wall_v)
    south_h = jnp.concatenate([zeros, north_h[:, :-1]], axis=1)
    south_u = jnp.concatenate([zeros, north_u[:, :-1]], axis=1)
    south_v = jnp.concatenate([wall_v, north_v[:, :-1]], axis=1)
    factor = time_step / own_a
    new_h = own_h - factor * (flux_h[1:] - flux_h[:-1] + north_h - south_h)
    new_u = (
        own_u - factor * (flux_u[1:] - flux_u[:-1] + north_u - south_u) + time_step * own_f * own_v
    )
    new_v = (
        own_v - factor * (flux_v[1:] - flux_v[:-1] + north_v - south_v) - time_step * own_f * own_u
    )
    return jnp.stack([new_h, new_u, new_v])


def edge_kernel(odd_ref, ini_h, ini_t, dep_h, dep_t, cor_h, cor_t, area_h, area_t, face_h, face_t, near_ref, far_ref):
    odd = odd_ref[0] == 1
    head = [ini_h[0], ini_h[1], ini_h[2], dep_h[...], cor_h[...], area_h[...], face_h[0], face_h[1]]
    tail = [ini_t[0], ini_t[1], ini_t[2], dep_t[...], cor_t[...], area_t[...], face_t[0], face_t[1]]
    for c in range(CHANNELS):
        near_ref[c] = jnp.where(odd, head[c], tail[c])
        far_ref[c] = jnp.where(odd, tail[c], head[c])


def edges(odd, initial, depth_field, coriolis, cell_area, face_len):
    rows, lanes = depth_field.shape
    last = rows // HALO - 1
    spec3 = lambda b: pl.BlockSpec((3, HALO, lanes), lambda i: (0, b, 0))
    spec2 = lambda b: pl.BlockSpec((HALO, lanes), lambda i: (b, 0))
    specf = lambda b: pl.BlockSpec((2, HALO, lanes), lambda i: (0, b, 0))
    out = jax.ShapeDtypeStruct((CHANNELS, HALO, lanes), jnp.float32)
    return pl.pallas_call(
        edge_kernel,
        out_shape=(out, out),
        in_specs=[
            pl.BlockSpec(memory_space=pltpu.SMEM),
            spec3(0), spec3(last), spec2(0), spec2(last), spec2(0), spec2(last),
            spec2(0), spec2(last), specf(0), specf(last),
        ],
        out_specs=(
            pl.BlockSpec((CHANNELS, HALO, lanes), lambda i: (0, 0, 0)),
            pl.BlockSpec((CHANNELS, HALO, lanes), lambda i: (0, 0, 0)),
        ),
        grid=(1,),
    )(odd, initial, initial, depth_field, depth_field, coriolis, coriolis, cell_area, cell_area, face_len, face_len)


def stencil_kernel(odd_ref, ini, dep, cor, area, face, near_in, far_in, final_ref, snap_ref, ext):
    own_rows = ini.shape[1]
    odd = odd_ref[0] == 1
    owns = [ini[0], ini[1], ini[2], dep[...], cor[...], area[...], face[0], face[1]]
    for c in range(CHANNELS):
        ext[c, :HALO] = jnp.where(odd, near_in[c], far_in[c])
        ext[c, HALO : HALO + own_rows] = owns[c]
        ext[c, HALO + own_rows :] = jnp.where(odd, far_in[c], near_in[c])
    rows, lanes = ext.shape[1], ext.shape[2]
    lane = lax.broadcasted_iota(jnp.int32, (rows, lanes), 1)
    top = lane == lanes - 1
    bottom = lane == 0

    def east(x):
        return pltpu.roll(x, rows - 1, 0)

    def west(x):
        return pltpu.roll(x, 1, 0)

    def up(x):
        return pltpu.roll(x, lanes - 1, 1)

    def down(x):
        return pltpu.roll(x, 1, 1)

    depth, rotation, cell, east_len, north_len = (ext[c] for c in range(3, CHANNELS))
    wave_x = jnp.sqrt(jnp.maximum(depth, east(depth)))
    depth_e = east(depth)
    depth_up = jnp.where(top, depth, up(depth))
    wave_y = jnp.sqrt(jnp.maximum(depth, depth_up))
    root_d = jnp.sqrt(depth)
    factor = time_step / cell
    height, speed_x, speed_y = ext[0], ext[1], ext[2]
    for number in range(STEPS):
        h_e, u_e, v_e = east(height), east(speed_x), east(speed_y)
        flux_h = east_len * (
            0.5 * (depth * speed_x + depth_e * u_e) - 0.5 * wave_x * (h_e - height)
        )
        flux_u = east_len * (0.5 * (height + h_e) - 0.5 * wave_x * (u_e - speed_x))
        flux_v = east_len * (-0.5 * wave_x * (v_e - speed_y))
        h_up = jnp.where(top, height, up(height))
        u_up = jnp.where(top, speed_x, up(speed_x))
        v_up = jnp.where(top, -speed_y, up(speed_y))
        north_h = north_len * (
            0.5 * (depth * speed_y + depth_up * v_up) - 0.5 * wave_y * (h_up - height)
        )
        north_u = north_len * (-0.5 * wave_y * (u_up - speed_x))
        north_v = north_len * (0.5 * (height + h_up) - 0.5 * wave_y * (v_up - speed_y))
        wall_v = north_len * (height - root_d * speed_y)
        south_h = jnp.where(bottom, 0.0, down(north_h))
        south_u = jnp.where(bottom, 0.0, down(north_u))
        south_v = jnp.where(bottom, wall_v, down(north_v))
        new_h = height - factor * (flux_h - west(flux_h) + north_h - south_h)
        new_u = (
            speed_x
            - factor * (flux_u - west(flux_u) + north_u - south_u)
            + time_step * rotation * speed_y
        )
        new_v = (
            speed_y
            - factor * (flux_v - west(flux_v) + north_v - south_v)
            - time_step * rotation * speed_x
        )
        height, speed_x, speed_y = new_h, new_u, new_v
        for half in range(lanes // 128):
            snap_ref[number, half] = height[
                HALO : HALO + own_rows, half * 128 : (half + 1) * 128
            ].astype(snap_ref.dtype)
    final_ref[0] = height[HALO : HALO + own_rows]
    final_ref[1] = speed_x[HALO : HALO + own_rows]
    final_ref[2] = speed_y[HALO : HALO + own_rows]


def stencil(odd, initial, depth_field, coriolis, cell_area, face_len, near_in, far_in):
    rows, lanes = depth_field.shape
    whole = lambda shape: pl.BlockSpec(shape, lambda: (0,) * len(shape))
    snap_shape = (STEPS, lanes // 128, rows, 128)
    return pl.pallas_call(
        stencil_kernel,
        out_shape=(
            jax.ShapeDtypeStruct((3, rows, lanes), jnp.float32),
            jax.ShapeDtypeStruct(snap_shape, jnp.bfloat16),
        ),
        in_specs=[
            pl.BlockSpec(memory_space=pltpu.SMEM),
            whole(initial.shape), whole(depth_field.shape), whole(coriolis.shape),
            whole(cell_area.shape), whole(face_len.shape), whole(near_in.shape), whole(far_in.shape),
        ],
        out_specs=(whole((3, rows, lanes)), whole(snap_shape)),
        scratch_shapes=[pltpu.VMEM((CHANNELS, rows + 2 * HALO, lanes), jnp.float32)],
    )(odd, initial, depth_field, coriolis, cell_area, face_len, near_in, far_in)


def halo_exchange(near, far, axis):
    count = lax.axis_size(axis)
    odd = lax.axis_index(axis) % 2 == 1
    near_in = lax.ppermute(near, axis, [(i, i ^ 1) for i in range(count)])
    far_in = lax.ppermute(
        far, axis, [(i, (i + 1) % count if i % 2 else (i - 1) % count) for i in range(count)]
    )
    return near_in, far_in


def on_device(initial, depth_field, coriolis, cell_area, face_len, owners, offsets, weights):
    odd = (lax.axis_index("tile") % 2).astype(jnp.int32).reshape(1)
    near, far = edges(odd, initial, depth_field, coriolis, cell_area, face_len)
    near_in, far_in = halo_exchange(near, far, "tile")
    halves = initial.shape[2] // 128
    grouped = weights.reshape((-1, halves) + weights.shape[1:])
    columns = initial.shape[1]
    lo, hi = STEPS, columns - STEPS
    per_column = halves * weights.shape[1]
    slot_count = weights.shape[0] * weights.shape[1]

    def contribute(snaps, grouped_part):
        part = jnp.einsum(
            "shck,chrkt->chrst", snaps, grouped_part, preferred_element_type=jnp.float32
        )
        return part.reshape(-1, STEPS * 128)

    _, inner_snaps = stencil(odd, initial, depth_field, coriolis, cell_area, face_len, near, far)
    inner = contribute(inner_snaps[:, :, lo:hi], grouped[lo:hi])
    edge_weights = jnp.concatenate([grouped[:lo], grouped[hi:]], axis=0)
    n_tile = lax.axis_size("tile")
    item = jnp.arange(slot_count, dtype=jnp.int32)
    own_owner = owners.reshape(-1)
    same = own_owner[:, None] == own_owner[None, :]
    rank = jnp.sum((same & (item[None, :] < item[:, None])).astype(jnp.int32), axis=1)
    slot = own_owner * CAP + rank
    pack = (jnp.arange(n_tile * CAP, dtype=jnp.int32)[:, None] == slot[None, :]).astype(
        jnp.float32
    )
    inner_send = jnp.dot(
        pack[:, lo * per_column : hi * per_column],
        inner,
        precision=lax.Precision.HIGHEST,
        preferred_element_type=jnp.float32,
    )
    fields, snaps = stencil(odd, initial, depth_field, coriolis, cell_area, face_len, near_in, far_in)
    edge = contribute(
        jnp.concatenate([snaps[:, :, :lo], snaps[:, :, hi:]], axis=2), edge_weights
    )
    edge_pack = jnp.concatenate(
        [pack[:, : lo * per_column], pack[:, hi * per_column :]], axis=1
    )
    send = inner_send + jnp.dot(
        edge_pack, edge, precision=lax.Precision.HIGHEST, preferred_element_type=jnp.float32
    )
    labels = jnp.dot(
        pack,
        offsets.reshape(-1, 1).astype(jnp.float32) + 1.0,
        precision=lax.Precision.HIGHEST,
        preferred_element_type=jnp.float32,
    ).reshape(n_tile, CAP) - 1.0
    label_row = jnp.pad(labels, ((0, 0), (0, 128 - CAP)))
    payload = jnp.concatenate([send.reshape(n_tile, CAP * STEPS * 128), label_row], axis=1)
    recv = lax.all_to_all(payload, "tile", 0, 0, tiled=True)
    recv_data = recv[:, : CAP * STEPS * 128].reshape(n_tile * CAP, STEPS * 128)
    recv_offset = recv[:, CAP * STEPS * 128 : CAP * STEPS * 128 + CAP].reshape(-1)
    unpack = (
        recv_offset[None, :] == jnp.arange(TB, dtype=jnp.float32)[:, None]
    ).astype(jnp.float32)
    gathered = jnp.einsum(
        "tq,qsk->tsk",
        unpack,
        recv_data.reshape(n_tile * CAP, STEPS, 128),
        precision=lax.Precision.HIGHEST,
        preferred_element_type=jnp.float32,
    )
    return (gathered, fields)


def solution(mesh):
    placed = (
        P(None, ("exp", "tile"), None),
        P(("exp", "tile"), None),
        P(("exp", "tile"), None),
        P(("exp", "tile"), None),
        P(None, ("exp", "tile"), None),
        P(("exp", "tile"), None),
        P(("exp", "tile"), None),
        P(("exp", "tile"), None, None, None),
    )
    return jax.shard_map(
        on_device,
        mesh=mesh,
        in_specs=placed,
        out_specs=(P(("exp", "tile"), None, None), P(None, ("exp", "tile"), None)),
        check_vma=False,
    )
```

```python
import jax
import jax.numpy as jnp
from jax import lax
from jax.sharding import PartitionSpec as P
from jax.experimental import pallas as pl
from jax.experimental.pallas import tpu as pltpu

STEPS = 4
TB = 16
CAP = 4
HALO = 8
CHANNELS = 8


time_step = 0.3


def with_halo(cells, sides, width):
    for axis, dim in sides:
        count = lax.axis_size(axis)
        head = lax.slice_in_dim(cells, 0, width, axis=dim)
        tail = lax.slice_in_dim(cells, cells.shape[dim] - width, cells.shape[dim], axis=dim)
        if count % 2 == 0:
            odd = lax.axis_index(axis) % 2 == 1
            near = lax.ppermute(
                jnp.where(odd, head, tail), axis, [(i, i ^ 1) for i in range(count)]
            )
            far = lax.ppermute(
                jnp.where(odd, tail, head),
                axis,
                [(i, (i + 1) % count if i % 2 else (i - 1) % count) for i in range(count)],
            )
            before = jnp.where(odd, near, far)
            after = jnp.where(odd, far, near)
        else:
            before = lax.ppermute(tail, axis, [(i, (i + 1) % count) for i in range(count)])
            after = lax.ppermute(head, axis, [((i + 1) % count, i) for i in range(count)])
        cells = jnp.concatenate([before, cells, after], axis=dim)
    return cells


def advance(fields, metric):
    height, speed_x, speed_y = (fields[0], fields[1], fields[2])
    depth, rotation, area, east_len, north_len = (
        metric[0],
        metric[1],
        metric[2],
        metric[3],
        metric[4],
    )
    wave_x = jnp.sqrt(jnp.maximum(depth[:-1], depth[1:]))
    edge = east_len[:-1]
    flux_h = edge * (
        0.5 * (depth[:-1] * speed_x[:-1] + depth[1:] * speed_x[1:])
        - 0.5 * wave_x * (height[1:] - height[:-1])
    )
    flux_u = edge * (0.5 * (height[:-1] + height[1:]) - 0.5 * wave_x * (speed_x[1:] - speed_x[:-1]))
    flux_v = edge * (-0.5 * wave_x * (speed_y[1:] - speed_y[:-1]))
    own_h = height[1:-1]
    own_u = speed_x[1:-1]
    own_v = speed_y[1:-1]
    own_d = depth[1:-1]
    own_f = rotation[1:-1]
    own_a = area[1:-1]
    own_n = north_len[1:-1]
    above_h = jnp.concatenate([own_h[:, 1:], own_h[:, -1:]], axis=1)
    above_u = jnp.concatenate([own_u[:, 1:], own_u[:, -1:]], axis=1)
    above_v = jnp.concatenate([own_v[:, 1:], -own_v[:, -1:]], axis=1)
    above_d = jnp.concatenate([own_d[:, 1:], own_d[:, -1:]], axis=1)
    wave_y = jnp.sqrt(jnp.maximum(own_d, above_d))
    north_h = own_n * (0.5 * (own_d * own_v + above_d * above_v) - 0.5 * wave_y * (above_h - own_h))
    north_u = own_n * (-0.5 * wave_y * (above_u - own_u))
    north_v = own_n * (0.5 * (own_h + above_h) - 0.5 * wave_y * (above_v - own_v))
    wall_v = own_n[:, :1] * (own_h[:, :1] - jnp.sqrt(own_d[:, :1]) * own_v[:, :1])
    zeros = jnp.zeros_like(wall_v)
    south_h = jnp.concatenate([zeros, north_h[:, :-1]], axis=1)
    south_u = jnp.concatenate([zeros, north_u[:, :-1]], axis=1)
    south_v = jnp.concatenate([wall_v, north_v[:, :-1]], axis=1)
    factor = time_step / own_a
    new_h = own_h - factor * (flux_h[1:] - flux_h[:-1] + north_h - south_h)
    new_u = (
        own_u - factor * (flux_u[1:] - flux_u[:-1] + north_u - south_u) + time_step * own_f * own_v
    )
    new_v = (
        own_v - factor * (flux_v[1:] - flux_v[:-1] + north_v - south_v) - time_step * own_f * own_u
    )
    return jnp.stack([new_h, new_u, new_v])


def edge_kernel(odd_ref, ini_h, ini_t, dep_h, dep_t, cor_h, cor_t, area_h, area_t, face_h, face_t, near_ref, far_ref):
    odd = odd_ref[0] == 1
    head = [ini_h[0], ini_h[1], ini_h[2], dep_h[...], cor_h[...], area_h[...], face_h[0], face_h[1]]
    tail = [ini_t[0], ini_t[1], ini_t[2], dep_t[...], cor_t[...], area_t[...], face_t[0], face_t[1]]
    for c in range(CHANNELS):
        near_ref[c] = jnp.where(odd, head[c], tail[c])
        far_ref[c] = jnp.where(odd, tail[c], head[c])


def edges(odd, initial, depth_field, coriolis, cell_area, face_len):
    rows, lanes = depth_field.shape
    last = rows // HALO - 1
    spec3 = lambda b: pl.BlockSpec((3, HALO, lanes), lambda i: (0, b, 0))
    spec2 = lambda b: pl.BlockSpec((HALO, lanes), lambda i: (b, 0))
    specf = lambda b: pl.BlockSpec((2, HALO, lanes), lambda i: (0, b, 0))
    out = jax.ShapeDtypeStruct((CHANNELS, HALO, lanes), jnp.float32)
    return pl.pallas_call(
        edge_kernel,
        out_shape=(out, out),
        in_specs=[
            pl.BlockSpec(memory_space=pltpu.SMEM),
            spec3(0), spec3(last), spec2(0), spec2(last), spec2(0), spec2(last),
            spec2(0), spec2(last), specf(0), specf(last),
        ],
        out_specs=(
            pl.BlockSpec((CHANNELS, HALO, lanes), lambda i: (0, 0, 0)),
            pl.BlockSpec((CHANNELS, HALO, lanes), lambda i: (0, 0, 0)),
        ),
        grid=(1,),
    )(odd, initial, initial, depth_field, depth_field, coriolis, coriolis, cell_area, cell_area, face_len, face_len)


def stencil_kernel(
    odd_ref, ini, dep, cor, area, face, near_in, far_in, final_ref, snap_ref, edge_ref, ext
):
    own_rows = ini.shape[1]
    odd = odd_ref[0] == 1
    owns = [ini[0], ini[1], ini[2], dep[...], cor[...], area[...], face[0], face[1]]
    for c in range(CHANNELS):
        ext[c, :HALO] = jnp.where(odd, near_in[c], far_in[c])
        ext[c, HALO : HALO + own_rows] = owns[c]
        ext[c, HALO + own_rows :] = jnp.where(odd, far_in[c], near_in[c])
    rows, lanes = ext.shape[1], ext.shape[2]
    lane = lax.broadcasted_iota(jnp.int32, (rows, lanes), 1)
    top = lane == lanes - 1
    bottom = lane == 0

    def east(x):
        return pltpu.roll(x, rows - 1, 0)

    def west(x):
        return pltpu.roll(x, 1, 0)

    def up(x):
        return pltpu.roll(x, lanes - 1, 1)

    def down(x):
        return pltpu.roll(x, 1, 1)

    depth, rotation, cell, east_len, north_len = (ext[c] for c in range(3, CHANNELS))
    wave_x = jnp.sqrt(jnp.maximum(depth, east(depth)))
    depth_e = east(depth)
    depth_up = jnp.where(top, depth, up(depth))
    wave_y = jnp.sqrt(jnp.maximum(depth, depth_up))
    root_d = jnp.sqrt(depth)
    factor = time_step / cell
    height, speed_x, speed_y = ext[0], ext[1], ext[2]
    for number in range(STEPS):
        h_e, u_e, v_e = east(height), east(speed_x), east(speed_y)
        flux_h = east_len * (
            0.5 * (depth * speed_x + depth_e * u_e) - 0.5 * wave_x * (h_e - height)
        )
        flux_u = east_len * (0.5 * (height + h_e) - 0.5 * wave_x * (u_e - speed_x))
        flux_v = east_len * (-0.5 * wave_x * (v_e - speed_y))
        h_up = jnp.where(top, height, up(height))
        u_up = jnp.where(top, speed_x, up(speed_x))
        v_up = jnp.where(top, -speed_y, up(speed_y))
        north_h = north_len * (
            0.5 * (depth * speed_y + depth_up * v_up) - 0.5 * wave_y * (h_up - height)
        )
        north_u = north_len * (-0.5 * wave_y * (u_up - speed_x))
        north_v = north_len * (0.5 * (height + h_up) - 0.5 * wave_y * (v_up - speed_y))
        wall_v = north_len * (height - root_d * speed_y)
        south_h = jnp.where(bottom, 0.0, down(north_h))
        south_u = jnp.where(bottom, 0.0, down(north_u))
        south_v = jnp.where(bottom, wall_v, down(north_v))
        new_h = height - factor * (flux_h - west(flux_h) + north_h - south_h)
        new_u = (
            speed_x
            - factor * (flux_u - west(flux_u) + north_u - south_u)
            + time_step * rotation * speed_y
        )
        new_v = (
            speed_y
            - factor * (flux_v - west(flux_v) + north_v - south_v)
            - time_step * rotation * speed_x
        )
        height, speed_x, speed_y = new_h, new_u, new_v
        for half in range(lanes // 128):
            snap_ref[number, half] = height[
                HALO : HALO + own_rows, half * 128 : (half + 1) * 128
            ].astype(snap_ref.dtype)
            rounded = height[:, half * 128 : (half + 1) * 128].astype(snap_ref.dtype)
            edge_ref[number, half, :STEPS] = rounded[HALO : HALO + STEPS].astype(jnp.float32)
            edge_ref[number, half, STEPS:] = rounded[
                HALO + own_rows - STEPS : HALO + own_rows
            ].astype(jnp.float32)
    final_ref[0] = height[HALO : HALO + own_rows]
    final_ref[1] = speed_x[HALO : HALO + own_rows]
    final_ref[2] = speed_y[HALO : HALO + own_rows]


def stencil(odd, initial, depth_field, coriolis, cell_area, face_len, near_in, far_in):
    rows, lanes = depth_field.shape
    whole = lambda shape: pl.BlockSpec(shape, lambda: (0,) * len(shape))
    snap_shape = (STEPS, lanes // 128, rows, 128)
    edge_shape = (STEPS, lanes // 128, 2 * STEPS, 128)
    return pl.pallas_call(
        stencil_kernel,
        out_shape=(
            jax.ShapeDtypeStruct((3, rows, lanes), jnp.float32),
            jax.ShapeDtypeStruct(snap_shape, jnp.bfloat16),
            jax.ShapeDtypeStruct(edge_shape, jnp.float32),
        ),
        in_specs=[
            pl.BlockSpec(memory_space=pltpu.SMEM),
            whole(initial.shape), whole(depth_field.shape), whole(coriolis.shape),
            whole(cell_area.shape), whole(face_len.shape), whole(near_in.shape), whole(far_in.shape),
        ],
        out_specs=(whole((3, rows, lanes)), whole(snap_shape), whole(edge_shape)),
        scratch_shapes=[pltpu.VMEM((CHANNELS, rows + 2 * HALO, lanes), jnp.float32)],
    )(odd, initial, depth_field, coriolis, cell_area, face_len, near_in, far_in)


def halo_exchange(near, far, axis):
    count = lax.axis_size(axis)
    odd = lax.axis_index(axis) % 2 == 1
    near_in = lax.ppermute(near, axis, [(i, i ^ 1) for i in range(count)])
    far_in = lax.ppermute(
        far, axis, [(i, (i + 1) % count if i % 2 else (i - 1) % count) for i in range(count)]
    )
    return near_in, far_in


def on_device(initial, depth_field, coriolis, cell_area, face_len, owners, offsets, weights):
    odd = (lax.axis_index("tile") % 2).astype(jnp.int32).reshape(1)
    near, far = edges(odd, initial, depth_field, coriolis, cell_area, face_len)
    near_in, far_in = halo_exchange(near, far, "tile")
    halves = initial.shape[2] // 128
    grouped = weights.reshape((-1, halves) + weights.shape[1:])
    columns = initial.shape[1]
    lo, hi = STEPS, columns - STEPS
    per_column = halves * weights.shape[1]
    slot_count = weights.shape[0] * weights.shape[1]

    def contribute(snaps, grouped_part):
        part = jnp.einsum(
            "shck,chrkt->chrst", snaps, grouped_part, preferred_element_type=jnp.float32
        )
        return part.reshape(-1, STEPS * 128)

    _, inner_snaps, _ = stencil(odd, initial, depth_field, coriolis, cell_area, face_len, near, far)
    inner = contribute(inner_snaps[:, :, lo:hi], grouped[lo:hi])
    edge_weights = jnp.concatenate([grouped[:lo], grouped[hi:]], axis=0)
    n_tile = lax.axis_size("tile")
    item = jnp.arange(slot_count, dtype=jnp.int32)
    own_owner = owners.reshape(-1)
    same = own_owner[:, None] == own_owner[None, :]
    rank = jnp.sum((same & (item[None, :] < item[:, None])).astype(jnp.int32), axis=1)
    slot = own_owner * CAP + rank
    pack = (jnp.arange(n_tile * CAP, dtype=jnp.int32)[:, None] == slot[None, :]).astype(
        jnp.float32
    )
    inner_send = jnp.dot(
        pack[:, lo * per_column : hi * per_column],
        inner,
        precision=lax.Precision.HIGHEST,
        preferred_element_type=jnp.float32,
    )
    fields, _, edge_snaps = stencil(
        odd, initial, depth_field, coriolis, cell_area, face_len, near_in, far_in
    )
    edge = contribute(edge_snaps.astype(jnp.bfloat16), edge_weights)
    edge_pack = jnp.concatenate(
        [pack[:, : lo * per_column], pack[:, hi * per_column :]], axis=1
    )
    send = inner_send + jnp.dot(
        edge_pack, edge, precision=lax.Precision.HIGHEST, preferred_element_type=jnp.float32
    )
    labels = jnp.dot(
        pack,
        offsets.reshape(-1, 1).astype(jnp.float32) + 1.0,
        precision=lax.Precision.HIGHEST,
        preferred_element_type=jnp.float32,
    ).reshape(n_tile, CAP) - 1.0
    label_row = jnp.pad(labels, ((0, 0), (0, 128 - CAP)))
    payload = jnp.concatenate([send.reshape(n_tile, CAP * STEPS * 128), label_row], axis=1)
    recv = lax.all_to_all(payload, "tile", 0, 0, tiled=True)
    recv_data = recv[:, : CAP * STEPS * 128].reshape(n_tile * CAP, STEPS * 128)
    recv_offset = recv[:, CAP * STEPS * 128 : CAP * STEPS * 128 + CAP].reshape(-1)
    unpack = (
        recv_offset[None, :] == jnp.arange(TB, dtype=jnp.float32)[:, None]
    ).astype(jnp.float32)
    gathered = jnp.einsum(
        "tq,qsk->tsk",
        unpack,
        recv_data.reshape(n_tile * CAP, STEPS, 128),
        precision=lax.Precision.HIGHEST,
        preferred_element_type=jnp.float32,
    )
    return (gathered, fields)


def solution(mesh):
    placed = (
        P(None, ("exp", "tile"), None),
        P(("exp", "tile"), None),
        P(("exp", "tile"), None),
        P(("exp", "tile"), None),
        P(None, ("exp", "tile"), None),
        P(("exp", "tile"), None),
        P(("exp", "tile"), None),
        P(("exp", "tile"), None, None, None),
    )
    return jax.shard_map(
        on_device,
        mesh=mesh,
        in_specs=placed,
        out_specs=(P(("exp", "tile"), None, None), P(None, ("exp", "tile"), None)),
        check_vma=False,
    )
```

```python
import jax
import jax.numpy as jnp
from jax import lax
from jax.sharding import PartitionSpec as P
from jax.experimental import pallas as pl
from jax.experimental.pallas import tpu as pltpu

STEPS = 4
TB = 16
CAP = 4
HALO = 8
CHANNELS = 8


time_step = 0.3


def with_halo(cells, sides, width):
    for axis, dim in sides:
        count = lax.axis_size(axis)
        head = lax.slice_in_dim(cells, 0, width, axis=dim)
        tail = lax.slice_in_dim(cells, cells.shape[dim] - width, cells.shape[dim], axis=dim)
        if count % 2 == 0:
            odd = lax.axis_index(axis) % 2 == 1
            near = lax.ppermute(
                jnp.where(odd, head, tail), axis, [(i, i ^ 1) for i in range(count)]
            )
            far = lax.ppermute(
                jnp.where(odd, tail, head),
                axis,
                [(i, (i + 1) % count if i % 2 else (i - 1) % count) for i in range(count)],
            )
            before = jnp.where(odd, near, far)
            after = jnp.where(odd, far, near)
        else:
            before = lax.ppermute(tail, axis, [(i, (i + 1) % count) for i in range(count)])
            after = lax.ppermute(head, axis, [((i + 1) % count, i) for i in range(count)])
        cells = jnp.concatenate([before, cells, after], axis=dim)
    return cells


def advance(fields, metric):
    height, speed_x, speed_y = (fields[0], fields[1], fields[2])
    depth, rotation, area, east_len, north_len = (
        metric[0],
        metric[1],
        metric[2],
        metric[3],
        metric[4],
    )
    wave_x = jnp.sqrt(jnp.maximum(depth[:-1], depth[1:]))
    edge = east_len[:-1]
    flux_h = edge * (
        0.5 * (depth[:-1] * speed_x[:-1] + depth[1:] * speed_x[1:])
        - 0.5 * wave_x * (height[1:] - height[:-1])
    )
    flux_u = edge * (0.5 * (height[:-1] + height[1:]) - 0.5 * wave_x * (speed_x[1:] - speed_x[:-1]))
    flux_v = edge * (-0.5 * wave_x * (speed_y[1:] - speed_y[:-1]))
    own_h = height[1:-1]
    own_u = speed_x[1:-1]
    own_v = speed_y[1:-1]
    own_d = depth[1:-1]
    own_f = rotation[1:-1]
    own_a = area[1:-1]
    own_n = north_len[1:-1]
    above_h = jnp.concatenate([own_h[:, 1:], own_h[:, -1:]], axis=1)
    above_u = jnp.concatenate([own_u[:, 1:], own_u[:, -1:]], axis=1)
    above_v = jnp.concatenate([own_v[:, 1:], -own_v[:, -1:]], axis=1)
    above_d = jnp.concatenate([own_d[:, 1:], own_d[:, -1:]], axis=1)
    wave_y = jnp.sqrt(jnp.maximum(own_d, above_d))
    north_h = own_n * (0.5 * (own_d * own_v + above_d * above_v) - 0.5 * wave_y * (above_h - own_h))
    north_u = own_n * (-0.5 * wave_y * (above_u - own_u))
    north_v = own_n * (0.5 * (own_h + above_h) - 0.5 * wave_y * (above_v - own_v))
    wall_v = own_n[:, :1] * (own_h[:, :1] - jnp.sqrt(own_d[:, :1]) * own_v[:, :1])
    zeros = jnp.zeros_like(wall_v)
    south_h = jnp.concatenate([zeros, north_h[:, :-1]], axis=1)
    south_u = jnp.concatenate([zeros, north_u[:, :-1]], axis=1)
    south_v = jnp.concatenate([wall_v, north_v[:, :-1]], axis=1)
    factor = time_step / own_a
    new_h = own_h - factor * (flux_h[1:] - flux_h[:-1] + north_h - south_h)
    new_u = (
        own_u - factor * (flux_u[1:] - flux_u[:-1] + north_u - south_u) + time_step * own_f * own_v
    )
    new_v = (
        own_v - factor * (flux_v[1:] - flux_v[:-1] + north_v - south_v) - time_step * own_f * own_u
    )
    return jnp.stack([new_h, new_u, new_v])


def edge_kernel(odd_ref, ini_h, ini_t, dep_h, dep_t, cor_h, cor_t, area_h, area_t, face_h, face_t, near_ref, far_ref):
    odd = odd_ref[0] == 1
    head = [ini_h[0], ini_h[1], ini_h[2], dep_h[...], cor_h[...], area_h[...], face_h[0], face_h[1]]
    tail = [ini_t[0], ini_t[1], ini_t[2], dep_t[...], cor_t[...], area_t[...], face_t[0], face_t[1]]
    for c in range(CHANNELS):
        near_ref[c] = jnp.where(odd, head[c], tail[c])
        far_ref[c] = jnp.where(odd, tail[c], head[c])


def edges(odd, initial, depth_field, coriolis, cell_area, face_len):
    rows, lanes = depth_field.shape
    last = rows // HALO - 1
    spec3 = lambda b: pl.BlockSpec((3, HALO, lanes), lambda i: (0, b, 0))
    spec2 = lambda b: pl.BlockSpec((HALO, lanes), lambda i: (b, 0))
    specf = lambda b: pl.BlockSpec((2, HALO, lanes), lambda i: (0, b, 0))
    out = jax.ShapeDtypeStruct((CHANNELS, HALO, lanes), jnp.float32)
    return pl.pallas_call(
        edge_kernel,
        out_shape=(out, out),
        in_specs=[
            pl.BlockSpec(memory_space=pltpu.SMEM),
            spec3(0), spec3(last), spec2(0), spec2(last), spec2(0), spec2(last),
            spec2(0), spec2(last), specf(0), specf(last),
        ],
        out_specs=(
            pl.BlockSpec((CHANNELS, HALO, lanes), lambda i: (0, 0, 0)),
            pl.BlockSpec((CHANNELS, HALO, lanes), lambda i: (0, 0, 0)),
        ),
        grid=(1,),
    )(odd, initial, initial, depth_field, depth_field, coriolis, coriolis, cell_area, cell_area, face_len, face_len)


def stencil_kernel(
    odd_ref, ini, dep, cor, area, face, near_in, far_in, final_ref, snap_ref, edge_ref, ext
):
    own_rows = ini.shape[1]
    odd = odd_ref[0] == 1
    owns = [ini[0], ini[1], ini[2], dep[...], cor[...], area[...], face[0], face[1]]
    for c in range(CHANNELS):
        ext[c, :HALO] = jnp.where(odd, near_in[c], far_in[c])
        ext[c, HALO : HALO + own_rows] = owns[c]
        ext[c, HALO + own_rows :] = jnp.where(odd, far_in[c], near_in[c])
    rows, lanes = ext.shape[1], ext.shape[2]
    lane = lax.broadcasted_iota(jnp.int32, (rows, lanes), 1)
    top = lane == lanes - 1
    bottom = lane == 0

    def east(x):
        return pltpu.roll(x, rows - 1, 0)

    def west(x):
        return pltpu.roll(x, 1, 0)

    def up(x):
        return pltpu.roll(x, lanes - 1, 1)

    def down(x):
        return pltpu.roll(x, 1, 1)

    depth, rotation, cell, east_len, north_len = (ext[c] for c in range(3, CHANNELS))
    wave_x = jnp.sqrt(jnp.maximum(depth, east(depth)))
    depth_e = east(depth)
    depth_up = jnp.where(top, depth, up(depth))
    wave_y = jnp.sqrt(jnp.maximum(depth, depth_up))
    root_d = jnp.sqrt(depth)
    factor = time_step / cell
    height, speed_x, speed_y = ext[0], ext[1], ext[2]
    for number in range(STEPS):
        h_e, u_e, v_e = east(height), east(speed_x), east(speed_y)
        flux_h = east_len * (
            0.5 * (depth * speed_x + depth_e * u_e) - 0.5 * wave_x * (h_e - height)
        )
        flux_u = east_len * (0.5 * (height + h_e) - 0.5 * wave_x * (u_e - speed_x))
        flux_v = east_len * (-0.5 * wave_x * (v_e - speed_y))
        h_up = jnp.where(top, height, up(height))
        u_up = jnp.where(top, speed_x, up(speed_x))
        v_up = jnp.where(top, -speed_y, up(speed_y))
        north_h = north_len * (
            0.5 * (depth * speed_y + depth_up * v_up) - 0.5 * wave_y * (h_up - height)
        )
        north_u = north_len * (-0.5 * wave_y * (u_up - speed_x))
        north_v = north_len * (0.5 * (height + h_up) - 0.5 * wave_y * (v_up - speed_y))
        wall_v = north_len * (height - root_d * speed_y)
        south_h = jnp.where(bottom, 0.0, down(north_h))
        south_u = jnp.where(bottom, 0.0, down(north_u))
        south_v = jnp.where(bottom, wall_v, down(north_v))
        new_h = height - factor * (flux_h - west(flux_h) + north_h - south_h)
        new_u = (
            speed_x
            - factor * (flux_u - west(flux_u) + north_u - south_u)
            + time_step * rotation * speed_y
        )
        new_v = (
            speed_y
            - factor * (flux_v - west(flux_v) + north_v - south_v)
            - time_step * rotation * speed_x
        )
        height, speed_x, speed_y = new_h, new_u, new_v
        for half in range(lanes // 128):
            snap_ref[number, half] = height[
                HALO : HALO + own_rows, half * 128 : (half + 1) * 128
            ].astype(snap_ref.dtype)
            rounded = height[:, half * 128 : (half + 1) * 128].astype(snap_ref.dtype)
            wide = rounded.astype(jnp.float32)
            for edge in range(2 * STEPS):
                row = HALO + edge if edge < STEPS else HALO + own_rows - 2 * STEPS + edge
                edge_ref[half, edge, pl.ds(number, 1), :] = wide[row : row + 1]
    final_ref[0] = height[HALO : HALO + own_rows]
    final_ref[1] = speed_x[HALO : HALO + own_rows]
    final_ref[2] = speed_y[HALO : HALO + own_rows]


def stencil(odd, initial, depth_field, coriolis, cell_area, face_len, near_in, far_in):
    rows, lanes = depth_field.shape
    whole = lambda shape: pl.BlockSpec(shape, lambda: (0,) * len(shape))
    snap_shape = (STEPS, lanes // 128, rows, 128)
    edge_shape = (lanes // 128, 2 * STEPS, 8, 128)
    return pl.pallas_call(
        stencil_kernel,
        out_shape=(
            jax.ShapeDtypeStruct((3, rows, lanes), jnp.float32),
            jax.ShapeDtypeStruct(snap_shape, jnp.bfloat16),
            jax.ShapeDtypeStruct(edge_shape, jnp.float32),
        ),
        in_specs=[
            pl.BlockSpec(memory_space=pltpu.SMEM),
            whole(initial.shape), whole(depth_field.shape), whole(coriolis.shape),
            whole(cell_area.shape), whole(face_len.shape), whole(near_in.shape), whole(far_in.shape),
        ],
        out_specs=(whole((3, rows, lanes)), whole(snap_shape), whole(edge_shape)),
        scratch_shapes=[pltpu.VMEM((CHANNELS, rows + 2 * HALO, lanes), jnp.float32)],
    )(odd, initial, depth_field, coriolis, cell_area, face_len, near_in, far_in)


def edge_contrib_kernel(edge_ref, weight_ref, out_ref):
    for block in range(weight_ref.shape[0]):
        for half in range(weight_ref.shape[1]):
            lhs = edge_ref[half, block].astype(jnp.bfloat16)
            for part in range(weight_ref.shape[2]):
                product = jnp.dot(
                    lhs, weight_ref[block, half, part], preferred_element_type=jnp.float32
                )
                out_ref[block, half, part] = product[:STEPS]


def edge_contrib(edge_snaps, edge_weights):
    whole = lambda shape: pl.BlockSpec(shape, lambda: (0,) * len(shape))
    blocks, halves, parts = edge_weights.shape[:3]
    shape = (blocks, halves, parts, STEPS, 128)
    return pl.pallas_call(
        edge_contrib_kernel,
        out_shape=jax.ShapeDtypeStruct(shape, jnp.float32),
        in_specs=[whole(edge_snaps.shape), whole(edge_weights.shape)],
        out_specs=whole(shape),
    )(edge_snaps, edge_weights)


def halo_exchange(near, far, axis):
    count = lax.axis_size(axis)
    odd = lax.axis_index(axis) % 2 == 1
    near_in = lax.ppermute(near, axis, [(i, i ^ 1) for i in range(count)])
    far_in = lax.ppermute(
        far, axis, [(i, (i + 1) % count if i % 2 else (i - 1) % count) for i in range(count)]
    )
    return near_in, far_in


def on_device(initial, depth_field, coriolis, cell_area, face_len, owners, offsets, weights):
    odd = (lax.axis_index("tile") % 2).astype(jnp.int32).reshape(1)
    near, far = edges(odd, initial, depth_field, coriolis, cell_area, face_len)
    near_in, far_in = halo_exchange(near, far, "tile")
    halves = initial.shape[2] // 128
    grouped = weights.reshape((-1, halves) + weights.shape[1:])
    columns = initial.shape[1]
    lo, hi = STEPS, columns - STEPS
    per_column = halves * weights.shape[1]
    slot_count = weights.shape[0] * weights.shape[1]

    def contribute(snaps, grouped_part):
        part = jnp.einsum(
            "shck,chrkt->chrst", snaps, grouped_part, preferred_element_type=jnp.float32
        )
        return part.reshape(-1, STEPS * 128)

    _, inner_snaps, _ = stencil(odd, initial, depth_field, coriolis, cell_area, face_len, near, far)
    inner = contribute(inner_snaps[:, :, lo:hi], grouped[lo:hi])
    edge_weights = jnp.concatenate([grouped[:lo], grouped[hi:]], axis=0)
    n_tile = lax.axis_size("tile")
    item = jnp.arange(slot_count, dtype=jnp.int32)
    own_owner = owners.reshape(-1)
    same = own_owner[:, None] == own_owner[None, :]
    rank = jnp.sum((same & (item[None, :] < item[:, None])).astype(jnp.int32), axis=1)
    slot = own_owner * CAP + rank
    pack = (jnp.arange(n_tile * CAP, dtype=jnp.int32)[:, None] == slot[None, :]).astype(
        jnp.float32
    )
    inner_send = jnp.dot(
        pack[:, lo * per_column : hi * per_column],
        inner,
        precision=lax.Precision.HIGHEST,
        preferred_element_type=jnp.float32,
    )
    fields, _, edge_snaps = stencil(
        odd, initial, depth_field, coriolis, cell_area, face_len, near_in, far_in
    )
    edge = edge_contrib(edge_snaps, edge_weights).reshape(-1, STEPS * 128)
    edge_pack = jnp.concatenate(
        [pack[:, : lo * per_column], pack[:, hi * per_column :]], axis=1
    )
    send = inner_send + jnp.dot(
        edge_pack, edge, precision=lax.Precision.HIGHEST, preferred_element_type=jnp.float32
    )
    labels = jnp.dot(
        pack,
        offsets.reshape(-1, 1).astype(jnp.float32) + 1.0,
        precision=lax.Precision.HIGHEST,
        preferred_element_type=jnp.float32,
    ).reshape(n_tile, CAP) - 1.0
    label_row = jnp.pad(labels, ((0, 0), (0, 128 - CAP)))
    payload = jnp.concatenate([send.reshape(n_tile, CAP * STEPS * 128), label_row], axis=1)
    recv = lax.all_to_all(payload, "tile", 0, 0, tiled=True)
    recv_data = recv[:, : CAP * STEPS * 128].reshape(n_tile * CAP, STEPS * 128)
    recv_offset = recv[:, CAP * STEPS * 128 : CAP * STEPS * 128 + CAP].reshape(-1)
    unpack = (
        recv_offset[None, :] == jnp.arange(TB, dtype=jnp.float32)[:, None]
    ).astype(jnp.float32)
    gathered = jnp.einsum(
        "tq,qsk->tsk",
        unpack,
        recv_data.reshape(n_tile * CAP, STEPS, 128),
        precision=lax.Precision.HIGHEST,
        preferred_element_type=jnp.float32,
    )
    return (gathered, fields)


def solution(mesh):
    placed = (
        P(None, ("exp", "tile"), None),
        P(("exp", "tile"), None),
        P(("exp", "tile"), None),
        P(("exp", "tile"), None),
        P(None, ("exp", "tile"), None),
        P(("exp", "tile"), None),
        P(("exp", "tile"), None),
        P(("exp", "tile"), None, None, None),
    )
    return jax.shard_map(
        on_device,
        mesh=mesh,
        in_specs=placed,
        out_specs=(P(("exp", "tile"), None, None), P(None, ("exp", "tile"), None)),
        check_vma=False,
    )
```

```python
import jax
import jax.numpy as jnp
from jax import lax
from jax.sharding import PartitionSpec as P
from jax.experimental import pallas as pl
from jax.experimental.pallas import tpu as pltpu

STEPS = 4
TB = 16
CAP = 4
HALO = 8
CHANNELS = 8


time_step = 0.3


def with_halo(cells, sides, width):
    for axis, dim in sides:
        count = lax.axis_size(axis)
        head = lax.slice_in_dim(cells, 0, width, axis=dim)
        tail = lax.slice_in_dim(cells, cells.shape[dim] - width, cells.shape[dim], axis=dim)
        if count % 2 == 0:
            odd = lax.axis_index(axis) % 2 == 1
            near = lax.ppermute(
                jnp.where(odd, head, tail), axis, [(i, i ^ 1) for i in range(count)]
            )
            far = lax.ppermute(
                jnp.where(odd, tail, head),
                axis,
                [(i, (i + 1) % count if i % 2 else (i - 1) % count) for i in range(count)],
            )
            before = jnp.where(odd, near, far)
            after = jnp.where(odd, far, near)
        else:
            before = lax.ppermute(tail, axis, [(i, (i + 1) % count) for i in range(count)])
            after = lax.ppermute(head, axis, [((i + 1) % count, i) for i in range(count)])
        cells = jnp.concatenate([before, cells, after], axis=dim)
    return cells


def advance(fields, metric):
    height, speed_x, speed_y = (fields[0], fields[1], fields[2])
    depth, rotation, area, east_len, north_len = (
        metric[0],
        metric[1],
        metric[2],
        metric[3],
        metric[4],
    )
    wave_x = jnp.sqrt(jnp.maximum(depth[:-1], depth[1:]))
    edge = east_len[:-1]
    flux_h = edge * (
        0.5 * (depth[:-1] * speed_x[:-1] + depth[1:] * speed_x[1:])
        - 0.5 * wave_x * (height[1:] - height[:-1])
    )
    flux_u = edge * (0.5 * (height[:-1] + height[1:]) - 0.5 * wave_x * (speed_x[1:] - speed_x[:-1]))
    flux_v = edge * (-0.5 * wave_x * (speed_y[1:] - speed_y[:-1]))
    own_h = height[1:-1]
    own_u = speed_x[1:-1]
    own_v = speed_y[1:-1]
    own_d = depth[1:-1]
    own_f = rotation[1:-1]
    own_a = area[1:-1]
    own_n = north_len[1:-1]
    above_h = jnp.concatenate([own_h[:, 1:], own_h[:, -1:]], axis=1)
    above_u = jnp.concatenate([own_u[:, 1:], own_u[:, -1:]], axis=1)
    above_v = jnp.concatenate([own_v[:, 1:], -own_v[:, -1:]], axis=1)
    above_d = jnp.concatenate([own_d[:, 1:], own_d[:, -1:]], axis=1)
    wave_y = jnp.sqrt(jnp.maximum(own_d, above_d))
    north_h = own_n * (0.5 * (own_d * own_v + above_d * above_v) - 0.5 * wave_y * (above_h - own_h))
    north_u = own_n * (-0.5 * wave_y * (above_u - own_u))
    north_v = own_n * (0.5 * (own_h + above_h) - 0.5 * wave_y * (above_v - own_v))
    wall_v = own_n[:, :1] * (own_h[:, :1] - jnp.sqrt(own_d[:, :1]) * own_v[:, :1])
    zeros = jnp.zeros_like(wall_v)
    south_h = jnp.concatenate([zeros, north_h[:, :-1]], axis=1)
    south_u = jnp.concatenate([zeros, north_u[:, :-1]], axis=1)
    south_v = jnp.concatenate([wall_v, north_v[:, :-1]], axis=1)
    factor = time_step / own_a
    new_h = own_h - factor * (flux_h[1:] - flux_h[:-1] + north_h - south_h)
    new_u = (
        own_u - factor * (flux_u[1:] - flux_u[:-1] + north_u - south_u) + time_step * own_f * own_v
    )
    new_v = (
        own_v - factor * (flux_v[1:] - flux_v[:-1] + north_v - south_v) - time_step * own_f * own_u
    )
    return jnp.stack([new_h, new_u, new_v])


def edge_kernel(odd_ref, ini_h, ini_t, dep_h, dep_t, cor_h, cor_t, area_h, area_t, face_h, face_t, near_ref, far_ref):
    odd = odd_ref[0] == 1
    head = [ini_h[0], ini_h[1], ini_h[2], dep_h[...], cor_h[...], area_h[...], face_h[0], face_h[1]]
    tail = [ini_t[0], ini_t[1], ini_t[2], dep_t[...], cor_t[...], area_t[...], face_t[0], face_t[1]]
    for c in range(CHANNELS):
        near_ref[c] = jnp.where(odd, head[c], tail[c])
        far_ref[c] = jnp.where(odd, tail[c], head[c])


def edges(odd, initial, depth_field, coriolis, cell_area, face_len):
    rows, lanes = depth_field.shape
    last = rows // HALO - 1
    spec3 = lambda b: pl.BlockSpec((3, HALO, lanes), lambda i: (0, b, 0))
    spec2 = lambda b: pl.BlockSpec((HALO, lanes), lambda i: (b, 0))
    specf = lambda b: pl.BlockSpec((2, HALO, lanes), lambda i: (0, b, 0))
    out = jax.ShapeDtypeStruct((CHANNELS, HALO, lanes), jnp.float32)
    return pl.pallas_call(
        edge_kernel,
        out_shape=(out, out),
        in_specs=[
            pl.BlockSpec(memory_space=pltpu.SMEM),
            spec3(0), spec3(last), spec2(0), spec2(last), spec2(0), spec2(last),
            spec2(0), spec2(last), specf(0), specf(last),
        ],
        out_specs=(
            pl.BlockSpec((CHANNELS, HALO, lanes), lambda i: (0, 0, 0)),
            pl.BlockSpec((CHANNELS, HALO, lanes), lambda i: (0, 0, 0)),
        ),
        grid=(1,),
    )(odd, initial, initial, depth_field, depth_field, coriolis, coriolis, cell_area, cell_area, face_len, face_len)


def stencil_kernel(
    odd_ref, ini, dep, cor, area, face, near_in, far_in, final_ref, snap_ref, edge_ref, ext
):
    own_rows = ini.shape[1]
    odd = odd_ref[0] == 1
    owns = [ini[0], ini[1], ini[2], dep[...], cor[...], area[...], face[0], face[1]]
    for c in range(CHANNELS):
        ext[c, :HALO] = jnp.where(odd, near_in[c], far_in[c])
        ext[c, HALO : HALO + own_rows] = owns[c]
        ext[c, HALO + own_rows :] = jnp.where(odd, far_in[c], near_in[c])
    rows, lanes = ext.shape[1], ext.shape[2]
    lane = lax.broadcasted_iota(jnp.int32, (rows, lanes), 1)
    top = lane == lanes - 1
    bottom = lane == 0

    def east(x):
        return pltpu.roll(x, rows - 1, 0)

    def west(x):
        return pltpu.roll(x, 1, 0)

    def up(x):
        return pltpu.roll(x, lanes - 1, 1)

    def down(x):
        return pltpu.roll(x, 1, 1)

    depth, rotation, cell, east_len, north_len = (ext[c] for c in range(3, CHANNELS))
    wave_x = jnp.sqrt(jnp.maximum(depth, east(depth)))
    depth_e = east(depth)
    depth_up = jnp.where(top, depth, up(depth))
    wave_y = jnp.sqrt(jnp.maximum(depth, depth_up))
    root_d = jnp.sqrt(depth)
    factor = time_step / cell
    height, speed_x, speed_y = ext[0], ext[1], ext[2]
    for number in range(STEPS):
        h_e, u_e, v_e = east(height), east(speed_x), east(speed_y)
        flux_h = east_len * (
            0.5 * (depth * speed_x + depth_e * u_e) - 0.5 * wave_x * (h_e - height)
        )
        flux_u = east_len * (0.5 * (height + h_e) - 0.5 * wave_x * (u_e - speed_x))
        flux_v = east_len * (-0.5 * wave_x * (v_e - speed_y))
        h_up = jnp.where(top, height, up(height))
        u_up = jnp.where(top, speed_x, up(speed_x))
        v_up = jnp.where(top, -speed_y, up(speed_y))
        north_h = north_len * (
            0.5 * (depth * speed_y + depth_up * v_up) - 0.5 * wave_y * (h_up - height)
        )
        north_u = north_len * (-0.5 * wave_y * (u_up - speed_x))
        north_v = north_len * (0.5 * (height + h_up) - 0.5 * wave_y * (v_up - speed_y))
        wall_v = north_len * (height - root_d * speed_y)
        south_h = jnp.where(bottom, 0.0, down(north_h))
        south_u = jnp.where(bottom, 0.0, down(north_u))
        south_v = jnp.where(bottom, wall_v, down(north_v))
        new_h = height - factor * (flux_h - west(flux_h) + north_h - south_h)
        new_u = (
            speed_x
            - factor * (flux_u - west(flux_u) + north_u - south_u)
            + time_step * rotation * speed_y
        )
        new_v = (
            speed_y
            - factor * (flux_v - west(flux_v) + north_v - south_v)
            - time_step * rotation * speed_x
        )
        height, speed_x, speed_y = new_h, new_u, new_v
        for half in range(lanes // 128):
            snap_ref[number, half] = height[
                HALO : HALO + own_rows, half * 128 : (half + 1) * 128
            ].astype(snap_ref.dtype)
            rounded = height[:, half * 128 : (half + 1) * 128].astype(snap_ref.dtype)
            edge_ref[number, half, :STEPS] = rounded[HALO : HALO + STEPS].astype(jnp.float32)
            edge_ref[number, half, STEPS:] = rounded[
                HALO + own_rows - STEPS : HALO + own_rows
            ].astype(jnp.float32)
    final_ref[0] = height[HALO : HALO + own_rows]
    final_ref[1] = speed_x[HALO : HALO + own_rows]
    final_ref[2] = speed_y[HALO : HALO + own_rows]


def stencil(odd, initial, depth_field, coriolis, cell_area, face_len, near_in, far_in, inner):
    rows, lanes = depth_field.shape
    whole = lambda shape: pl.BlockSpec(shape, lambda: (0,) * len(shape))
    shapes = [
        ((3, rows, lanes), jnp.float32),
        ((STEPS, lanes // 128, rows, 128), jnp.bfloat16),
        ((STEPS, lanes // 128, 2 * STEPS, 128), jnp.float32),
    ]
    kept = [1] if inner else [0, 2]
    dropped = [i for i in range(3) if i not in kept]

    def kernel(*refs):
        ins, outs, rest = refs[:8], refs[8 : 8 + len(kept)], refs[8 + len(kept) :]
        slots = [None] * 3
        for i, ref in zip(kept, outs):
            slots[i] = ref
        for i, ref in zip(dropped, rest[1:]):
            slots[i] = ref
        stencil_kernel(*ins, *slots, rest[0])

    return pl.pallas_call(
        kernel,
        out_shape=tuple(jax.ShapeDtypeStruct(*shapes[i]) for i in kept),
        in_specs=[
            pl.BlockSpec(memory_space=pltpu.SMEM),
            whole(initial.shape), whole(depth_field.shape), whole(coriolis.shape),
            whole(cell_area.shape), whole(face_len.shape), whole(near_in.shape), whole(far_in.shape),
        ],
        out_specs=tuple(whole(shapes[i][0]) for i in kept),
        scratch_shapes=[pltpu.VMEM((CHANNELS, rows + 2 * HALO, lanes), jnp.float32)]
        + [pltpu.VMEM(*shapes[i]) for i in dropped],
    )(odd, initial, depth_field, coriolis, cell_area, face_len, near_in, far_in)


def halo_exchange(near, far, axis):
    count = lax.axis_size(axis)
    odd = lax.axis_index(axis) % 2 == 1
    near_in = lax.ppermute(near, axis, [(i, i ^ 1) for i in range(count)])
    far_in = lax.ppermute(
        far, axis, [(i, (i + 1) % count if i % 2 else (i - 1) % count) for i in range(count)]
    )
    return near_in, far_in


def on_device(initial, depth_field, coriolis, cell_area, face_len, owners, offsets, weights):
    odd = (lax.axis_index("tile") % 2).astype(jnp.int32).reshape(1)
    near, far = edges(odd, initial, depth_field, coriolis, cell_area, face_len)
    near_in, far_in = halo_exchange(near, far, "tile")
    halves = initial.shape[2] // 128
    grouped = weights.reshape((-1, halves) + weights.shape[1:])
    columns = initial.shape[1]
    lo, hi = STEPS, columns - STEPS
    per_column = halves * weights.shape[1]
    slot_count = weights.shape[0] * weights.shape[1]

    def contribute(snaps, grouped_part):
        part = jnp.einsum(
            "shck,chrkt->chrst", snaps, grouped_part, preferred_element_type=jnp.float32
        )
        return part.reshape(-1, STEPS * 128)

    (inner_snaps,) = stencil(
        odd, initial, depth_field, coriolis, cell_area, face_len, near, far, True
    )
    inner = contribute(inner_snaps[:, :, lo:hi], grouped[lo:hi])
    edge_weights = jnp.concatenate([grouped[:lo], grouped[hi:]], axis=0)
    n_tile = lax.axis_size("tile")
    item = jnp.arange(slot_count, dtype=jnp.int32)
    own_owner = owners.reshape(-1)
    same = own_owner[:, None] == own_owner[None, :]
    rank = jnp.sum((same & (item[None, :] < item[:, None])).astype(jnp.int32), axis=1)
    slot = own_owner * CAP + rank
    pack = (jnp.arange(n_tile * CAP, dtype=jnp.int32)[:, None] == slot[None, :]).astype(
        jnp.float32
    )
    inner_send = jnp.dot(
        pack[:, lo * per_column : hi * per_column],
        inner,
        precision=lax.Precision.HIGHEST,
        preferred_element_type=jnp.float32,
    )
    fields, edge_snaps = stencil(
        odd, initial, depth_field, coriolis, cell_area, face_len, near_in, far_in, False
    )
    edge = contribute(edge_snaps.astype(jnp.bfloat16), edge_weights)
    edge_pack = jnp.concatenate(
        [pack[:, : lo * per_column], pack[:, hi * per_column :]], axis=1
    )
    send = inner_send + jnp.dot(
        edge_pack, edge, precision=lax.Precision.HIGHEST, preferred_element_type=jnp.float32
    )
    labels = jnp.dot(
        pack,
        offsets.reshape(-1, 1).astype(jnp.float32) + 1.0,
        precision=lax.Precision.HIGHEST,
        preferred_element_type=jnp.float32,
    ).reshape(n_tile, CAP) - 1.0
    label_row = jnp.pad(labels, ((0, 0), (0, 128 - CAP)))
    payload = jnp.concatenate([send.reshape(n_tile, CAP * STEPS * 128), label_row], axis=1)
    recv = lax.all_to_all(payload, "tile", 0, 0, tiled=True)
    recv_data = recv[:, : CAP * STEPS * 128].reshape(n_tile * CAP, STEPS * 128)
    recv_offset = recv[:, CAP * STEPS * 128 : CAP * STEPS * 128 + CAP].reshape(-1)
    unpack = (
        recv_offset[None, :] == jnp.arange(TB, dtype=jnp.float32)[:, None]
    ).astype(jnp.float32)
    gathered = jnp.einsum(
        "tq,qsk->tsk",
        unpack,
        recv_data.reshape(n_tile * CAP, STEPS, 128),
        precision=lax.Precision.HIGHEST,
        preferred_element_type=jnp.float32,
    )
    return (gathered, fields)


def solution(mesh):
    placed = (
        P(None, ("exp", "tile"), None),
        P(("exp", "tile"), None),
        P(("exp", "tile"), None),
        P(("exp", "tile"), None),
        P(None, ("exp", "tile"), None),
        P(("exp", "tile"), None),
        P(("exp", "tile"), None),
        P(("exp", "tile"), None, None, None),
    )
    return jax.shard_map(
        on_device,
        mesh=mesh,
        in_specs=placed,
        out_specs=(P(("exp", "tile"), None, None), P(None, ("exp", "tile"), None)),
        check_vma=False,
    )
```

```python
import jax
import jax.numpy as jnp
from jax import lax
from jax.sharding import PartitionSpec as P
from jax.experimental import pallas as pl
from jax.experimental.pallas import tpu as pltpu

STEPS = 4
TB = 16
CAP = 4
HALO = 8
CHANNELS = 8


time_step = 0.3


def with_halo(cells, sides, width):
    for axis, dim in sides:
        count = lax.axis_size(axis)
        head = lax.slice_in_dim(cells, 0, width, axis=dim)
        tail = lax.slice_in_dim(cells, cells.shape[dim] - width, cells.shape[dim], axis=dim)
        if count % 2 == 0:
            odd = lax.axis_index(axis) % 2 == 1
            near = lax.ppermute(
                jnp.where(odd, head, tail), axis, [(i, i ^ 1) for i in range(count)]
            )
            far = lax.ppermute(
                jnp.where(odd, tail, head),
                axis,
                [(i, (i + 1) % count if i % 2 else (i - 1) % count) for i in range(count)],
            )
            before = jnp.where(odd, near, far)
            after = jnp.where(odd, far, near)
        else:
            before = lax.ppermute(tail, axis, [(i, (i + 1) % count) for i in range(count)])
            after = lax.ppermute(head, axis, [((i + 1) % count, i) for i in range(count)])
        cells = jnp.concatenate([before, cells, after], axis=dim)
    return cells


def advance(fields, metric):
    height, speed_x, speed_y = (fields[0], fields[1], fields[2])
    depth, rotation, area, east_len, north_len = (
        metric[0],
        metric[1],
        metric[2],
        metric[3],
        metric[4],
    )
    wave_x = jnp.sqrt(jnp.maximum(depth[:-1], depth[1:]))
    edge = east_len[:-1]
    flux_h = edge * (
        0.5 * (depth[:-1] * speed_x[:-1] + depth[1:] * speed_x[1:])
        - 0.5 * wave_x * (height[1:] - height[:-1])
    )
    flux_u = edge * (0.5 * (height[:-1] + height[1:]) - 0.5 * wave_x * (speed_x[1:] - speed_x[:-1]))
    flux_v = edge * (-0.5 * wave_x * (speed_y[1:] - speed_y[:-1]))
    own_h = height[1:-1]
    own_u = speed_x[1:-1]
    own_v = speed_y[1:-1]
    own_d = depth[1:-1]
    own_f = rotation[1:-1]
    own_a = area[1:-1]
    own_n = north_len[1:-1]
    above_h = jnp.concatenate([own_h[:, 1:], own_h[:, -1:]], axis=1)
    above_u = jnp.concatenate([own_u[:, 1:], own_u[:, -1:]], axis=1)
    above_v = jnp.concatenate([own_v[:, 1:], -own_v[:, -1:]], axis=1)
    above_d = jnp.concatenate([own_d[:, 1:], own_d[:, -1:]], axis=1)
    wave_y = jnp.sqrt(jnp.maximum(own_d, above_d))
    north_h = own_n * (0.5 * (own_d * own_v + above_d * above_v) - 0.5 * wave_y * (above_h - own_h))
    north_u = own_n * (-0.5 * wave_y * (above_u - own_u))
    north_v = own_n * (0.5 * (own_h + above_h) - 0.5 * wave_y * (above_v - own_v))
    wall_v = own_n[:, :1] * (own_h[:, :1] - jnp.sqrt(own_d[:, :1]) * own_v[:, :1])
    zeros = jnp.zeros_like(wall_v)
    south_h = jnp.concatenate([zeros, north_h[:, :-1]], axis=1)
    south_u = jnp.concatenate([zeros, north_u[:, :-1]], axis=1)
    south_v = jnp.concatenate([wall_v, north_v[:, :-1]], axis=1)
    factor = time_step / own_a
    new_h = own_h - factor * (flux_h[1:] - flux_h[:-1] + north_h - south_h)
    new_u = (
        own_u - factor * (flux_u[1:] - flux_u[:-1] + north_u - south_u) + time_step * own_f * own_v
    )
    new_v = (
        own_v - factor * (flux_v[1:] - flux_v[:-1] + north_v - south_v) - time_step * own_f * own_u
    )
    return jnp.stack([new_h, new_u, new_v])


def edge_kernel(odd_ref, ini_h, ini_t, dep_h, dep_t, cor_h, cor_t, area_h, area_t, face_h, face_t, near_ref, far_ref):
    odd = odd_ref[0] == 1
    head = [ini_h[0], ini_h[1], ini_h[2], dep_h[...], cor_h[...], area_h[...], face_h[0], face_h[1]]
    tail = [ini_t[0], ini_t[1], ini_t[2], dep_t[...], cor_t[...], area_t[...], face_t[0], face_t[1]]
    for c in range(CHANNELS):
        near_ref[c] = jnp.where(odd, head[c], tail[c])
        far_ref[c] = jnp.where(odd, tail[c], head[c])


def edges(odd, initial, depth_field, coriolis, cell_area, face_len):
    rows, lanes = depth_field.shape
    last = rows // HALO - 1
    spec3 = lambda b: pl.BlockSpec((3, HALO, lanes), lambda i: (0, b, 0))
    spec2 = lambda b: pl.BlockSpec((HALO, lanes), lambda i: (b, 0))
    specf = lambda b: pl.BlockSpec((2, HALO, lanes), lambda i: (0, b, 0))
    out = jax.ShapeDtypeStruct((CHANNELS, HALO, lanes), jnp.float32)
    return pl.pallas_call(
        edge_kernel,
        out_shape=(out, out),
        in_specs=[
            pl.BlockSpec(memory_space=pltpu.SMEM),
            spec3(0), spec3(last), spec2(0), spec2(last), spec2(0), spec2(last),
            spec2(0), spec2(last), specf(0), specf(last),
        ],
        out_specs=(
            pl.BlockSpec((CHANNELS, HALO, lanes), lambda i: (0, 0, 0)),
            pl.BlockSpec((CHANNELS, HALO, lanes), lambda i: (0, 0, 0)),
        ),
        grid=(1,),
    )(odd, initial, initial, depth_field, depth_field, coriolis, coriolis, cell_area, cell_area, face_len, face_len)


def stencil_kernel(odd_ref, ini, dep, cor, area, face, near_in, far_in, final_ref, snap_ref, ext):
    own_rows = ini.shape[1]
    odd = odd_ref[0] == 1
    owns = [ini[0], ini[1], ini[2], dep[...], cor[...], area[...], face[0], face[1]]
    for c in range(CHANNELS):
        ext[c, :HALO] = jnp.where(odd, near_in[c], far_in[c])
        ext[c, HALO : HALO + own_rows] = owns[c]
        ext[c, HALO + own_rows :] = jnp.where(odd, far_in[c], near_in[c])
    rows, lanes = ext.shape[1], ext.shape[2]
    lane = lax.broadcasted_iota(jnp.int32, (rows, lanes), 1)
    top = lane == lanes - 1
    bottom = lane == 0

    def east(x):
        return pltpu.roll(x, rows - 1, 0)

    def west(x):
        return pltpu.roll(x, 1, 0)

    def up(x):
        return pltpu.roll(x, lanes - 1, 1)

    def down(x):
        return pltpu.roll(x, 1, 1)

    depth, rotation, cell, east_len, north_len = (ext[c] for c in range(3, CHANNELS))
    wave_x = jnp.sqrt(jnp.maximum(depth, east(depth)))
    depth_e = east(depth)
    depth_up = jnp.where(top, depth, up(depth))
    wave_y = jnp.sqrt(jnp.maximum(depth, depth_up))
    root_d = jnp.sqrt(depth)
    factor = time_step / cell
    height, speed_x, speed_y = ext[0], ext[1], ext[2]
    for number in range(STEPS):
        h_e, u_e, v_e = east(height), east(speed_x), east(speed_y)
        flux_h = east_len * (
            0.5 * (depth * speed_x + depth_e * u_e) - 0.5 * wave_x * (h_e - height)
        )
        flux_u = east_len * (0.5 * (height + h_e) - 0.5 * wave_x * (u_e - speed_x))
        flux_v = east_len * (-0.5 * wave_x * (v_e - speed_y))
        h_up = jnp.where(top, height, up(height))
        u_up = jnp.where(top, speed_x, up(speed_x))
        v_up = jnp.where(top, -speed_y, up(speed_y))
        north_h = north_len * (
            0.5 * (depth * speed_y + depth_up * v_up) - 0.5 * wave_y * (h_up - height)
        )
        north_u = north_len * (-0.5 * wave_y * (u_up - speed_x))
        north_v = north_len * (0.5 * (height + h_up) - 0.5 * wave_y * (v_up - speed_y))
        wall_v = north_len * (height - root_d * speed_y)
        south_h = jnp.where(bottom, 0.0, down(north_h))
        south_u = jnp.where(bottom, 0.0, down(north_u))
        south_v = jnp.where(bottom, wall_v, down(north_v))
        new_h = height - factor * (flux_h - west(flux_h) + north_h - south_h)
        new_u = (
            speed_x
            - factor * (flux_u - west(flux_u) + north_u - south_u)
            + time_step * rotation * speed_y
        )
        new_v = (
            speed_y
            - factor * (flux_v - west(flux_v) + north_v - south_v)
            - time_step * rotation * speed_x
        )
        height, speed_x, speed_y = new_h, new_u, new_v
        for half in range(lanes // 128):
            snap_ref[number, half] = height[
                HALO : HALO + own_rows, half * 128 : (half + 1) * 128
            ].astype(snap_ref.dtype)
    final_ref[0] = height[HALO : HALO + own_rows]
    final_ref[1] = speed_x[HALO : HALO + own_rows]
    final_ref[2] = speed_y[HALO : HALO + own_rows]


def stencil(odd, initial, depth_field, coriolis, cell_area, face_len, near_in, far_in, inner):
    rows, lanes = depth_field.shape
    whole = lambda shape: pl.BlockSpec(shape, lambda: (0,) * len(shape))
    final_shape = ((3, rows, lanes), jnp.float32)
    snap_shape = ((STEPS, lanes // 128, rows, 128), jnp.bfloat16)
    kept = [snap_shape] if inner else [final_shape, snap_shape]

    def kernel(*refs):
        if inner:
            stencil_kernel(*refs[:8], refs[10], refs[8], refs[9])
        else:
            stencil_kernel(*refs)

    return pl.pallas_call(
        kernel,
        out_shape=tuple(jax.ShapeDtypeStruct(*k) for k in kept),
        in_specs=[
            pl.BlockSpec(memory_space=pltpu.SMEM),
            whole(initial.shape), whole(depth_field.shape), whole(coriolis.shape),
            whole(cell_area.shape), whole(face_len.shape), whole(near_in.shape), whole(far_in.shape),
        ],
        out_specs=tuple(whole(k[0]) for k in kept),
        scratch_shapes=[pltpu.VMEM((CHANNELS, rows + 2 * HALO, lanes), jnp.float32)]
        + ([pltpu.VMEM(*final_shape)] if inner else []),
    )(odd, initial, depth_field, coriolis, cell_area, face_len, near_in, far_in)


def halo_exchange(near, far, axis):
    count = lax.axis_size(axis)
    odd = lax.axis_index(axis) % 2 == 1
    near_in = lax.ppermute(near, axis, [(i, i ^ 1) for i in range(count)])
    far_in = lax.ppermute(
        far, axis, [(i, (i + 1) % count if i % 2 else (i - 1) % count) for i in range(count)]
    )
    return near_in, far_in


def on_device(initial, depth_field, coriolis, cell_area, face_len, owners, offsets, weights):
    odd = (lax.axis_index("tile") % 2).astype(jnp.int32).reshape(1)
    near, far = edges(odd, initial, depth_field, coriolis, cell_area, face_len)
    near_in, far_in = halo_exchange(near, far, "tile")
    halves = initial.shape[2] // 128
    grouped = weights.reshape((-1, halves) + weights.shape[1:])
    columns = initial.shape[1]
    lo, hi = STEPS, columns - STEPS
    per_column = halves * weights.shape[1]
    slot_count = weights.shape[0] * weights.shape[1]

    def contribute(snaps, grouped_part):
        part = jnp.einsum(
            "shck,chrkt->chrst", snaps, grouped_part, preferred_element_type=jnp.float32
        )
        return part.reshape(-1, STEPS * 128)

    (inner_snaps,) = stencil(
        odd, initial, depth_field, coriolis, cell_area, face_len, near, far, True
    )
    inner = contribute(inner_snaps[:, :, lo:hi], grouped[lo:hi])
    edge_weights = jnp.concatenate([grouped[:lo], grouped[hi:]], axis=0)
    n_tile = lax.axis_size("tile")
    item = jnp.arange(slot_count, dtype=jnp.int32)
    own_owner = owners.reshape(-1)
    same = own_owner[:, None] == own_owner[None, :]
    rank = jnp.sum((same & (item[None, :] < item[:, None])).astype(jnp.int32), axis=1)
    slot = own_owner * CAP + rank
    pack = (jnp.arange(n_tile * CAP, dtype=jnp.int32)[:, None] == slot[None, :]).astype(
        jnp.float32
    )
    inner_send = jnp.dot(
        pack[:, lo * per_column : hi * per_column],
        inner,
        precision=lax.Precision.HIGHEST,
        preferred_element_type=jnp.float32,
    )
    fields, snaps = stencil(
        odd, initial, depth_field, coriolis, cell_area, face_len, near_in, far_in, False
    )
    edge = contribute(
        jnp.concatenate([snaps[:, :, :lo], snaps[:, :, hi:]], axis=2), edge_weights
    )
    edge_pack = jnp.concatenate(
        [pack[:, : lo * per_column], pack[:, hi * per_column :]], axis=1
    )
    send = inner_send + jnp.dot(
        edge_pack, edge, precision=lax.Precision.HIGHEST, preferred_element_type=jnp.float32
    )
    labels = jnp.dot(
        pack,
        offsets.reshape(-1, 1).astype(jnp.float32) + 1.0,
        precision=lax.Precision.HIGHEST,
        preferred_element_type=jnp.float32,
    ).reshape(n_tile, CAP) - 1.0
    label_row = jnp.pad(labels, ((0, 0), (0, 128 - CAP)))
    payload = jnp.concatenate([send.reshape(n_tile, CAP * STEPS * 128), label_row], axis=1)
    recv = lax.all_to_all(payload, "tile", 0, 0, tiled=True)
    recv_data = recv[:, : CAP * STEPS * 128].reshape(n_tile * CAP, STEPS * 128)
    recv_offset = recv[:, CAP * STEPS * 128 : CAP * STEPS * 128 + CAP].reshape(-1)
    unpack = (
        recv_offset[None, :] == jnp.arange(TB, dtype=jnp.float32)[:, None]
    ).astype(jnp.float32)
    gathered = jnp.einsum(
        "tq,qsk->tsk",
        unpack,
        recv_data.reshape(n_tile * CAP, STEPS, 128),
        precision=lax.Precision.HIGHEST,
        preferred_element_type=jnp.float32,
    )
    return (gathered, fields)


def solution(mesh):
    placed = (
        P(None, ("exp", "tile"), None),
        P(("exp", "tile"), None),
        P(("exp", "tile"), None),
        P(("exp", "tile"), None),
        P(None, ("exp", "tile"), None),
        P(("exp", "tile"), None),
        P(("exp", "tile"), None),
        P(("exp", "tile"), None, None, None),
    )
    return jax.shard_map(
        on_device,
        mesh=mesh,
        in_specs=placed,
        out_specs=(P(("exp", "tile"), None, None), P(None, ("exp", "tile"), None)),
        check_vma=False,
    )
```
